32 devices in a mesh: gz: 4 (over x, core), yx: 8 (over z, y).
Axes of the slice: x: 2, y: 2, z: 4, core: 2. Of those that a mesh axis runs over, the one named last changes fastest.
Arguments:
- features: bfloat16 [16, 64, 128, 128], P(None, 'gz', 'yx'), may hold values from -19 to 19
- conv_weight: bfloat16 [3, 16, 3, 3, 3], replicated, may hold values from -0.3125 to 0.3125
- conv_bias: float32 [3], replicated, may hold values from -3 to 3
- labels: int32 [64, 128, 128], P('gz', 'yx'), may hold values from 0 to 8, as said below
Outputs:
- probabilities: float32 [8, 64, 128, 128], P(None, 'gz', 'yx')
- affinities: float32 [3, 64, 128, 128], P(None, 'gz', 'yx')
The draws below stay inside these ranges and needn't reach their ends.
Inputs may be any that keep to these rules, and one draw needn't show every extreme that they name: `labels`: 0 marks an unseeded voxel, k marks a seed of colour k.
All inputs are finite; a program needn't handle non-finite values.
Results may differ from the reference program's by a relative error of at most 0.0012.
Values may be sent and summed in bfloat16 or wider, within the bound.
No kernel may reach another device: no remote copies, remote signals or barrier semaphores. Data moves between devices by JAX's collectives and lax.ppermute only.
A program may use at most 64 MiB of HBM per device.

```python
import jax
import jax.numpy as jnp
from jax import lax

CH = 16
FIELDS = 8
ITERS = 3
X = 128
NZ = 64
NY = 128


def draw_features(key, part):
    draw_shape = (CH, NZ, NY, X)
    depth_pos = jnp.arange(NZ, dtype=jnp.float32) / (NZ - 1)
    z_scale = (1.0 + 2.0 * depth_pos)[None, :, None, None]
    base_draw = jnp.clip(jax.random.normal(key, draw_shape, jnp.float32), -6.0, 6.0)
    values = base_draw * z_scale
    return values.astype(jnp.bfloat16)


def draw_labels(key, part):
    raw_values = jax.random.randint(key, (NZ, NY, X), 0, 64)
    colours = jnp.where(raw_values < 8, raw_values + 1, 0).astype(jnp.int32)
    return colours.at[0, 0, 0].set(8)


def noise(stream_key, shape, spread, limit, held_as=jnp.bfloat16):
    result = spread * jax.random.normal(stream_key, shape, jnp.float32)
    return jnp.clip(result, min=-limit, max=limit).astype(held_as)


def setup_inputs(seed: int = 0) -> dict:
    seeds = jax.random.split(jax.random.key(seed), 5)
    features = draw_features(jax.random.fold_in(seeds[4], 71), 0)
    conv_weight = noise(seeds[1], (3, CH, 3, 3, 3), (27 * CH) ** -0.5, 0.3125)
    conv_bias = noise(seeds[2], (3,), 1.0, 3.0, jnp.float32)
    labels = draw_labels(jax.random.fold_in(seeds[4], 71), 0)
    return {"features": features, "conv_weight": conv_weight, "conv_bias": conv_bias, "labels": labels}


RIDGE_WEIGHT = 0.5


def affinity_head(features, conv_weight, conv_bias):
    padded = jnp.pad(features, ((0, 0), (1, 1), (1, 1), (1, 1)))
    kernel = conv_weight.astype(jnp.float32)

    def plane_out(depth):
        slab_block = lax.dynamic_slice_in_dim(padded, depth, 3, 1).astype(jnp.float32)
        summed = jnp.zeros((3, NY, X), jnp.float32)
        for offset_z in range(3):
            for offset_y in range(3):
                for offset_x in range(3):
                    window = slab_block[:, offset_z, offset_y:offset_y + NY, offset_x:offset_x + X]
                    summed = summed + jnp.einsum("oc,cyx->oyx", kernel[:, :, offset_z, offset_y, offset_x], window, precision=lax.Precision.HIGHEST)
        return summed

    response = lax.map(plane_out, jnp.arange(NZ, dtype=jnp.int32))
    response = jnp.moveaxis(response, 0, 1)
    return jax.nn.sigmoid(response + conv_bias[:, None, None, None])


def edge_weights(affinities):
    keep_z = (jnp.arange(NZ, dtype=jnp.int32) < NZ - 1).astype(jnp.float32)[:, None, None]
    keep_y = (jnp.arange(NY, dtype=jnp.int32) < NY - 1).astype(jnp.float32)[None, :, None]
    keep_x = (jnp.arange(X, dtype=jnp.int32) < X - 1).astype(jnp.float32)[None, None, :]
    weight_zup = affinities[0] * keep_z
    weight_yup = affinities[1] * keep_y
    weight_xup = affinities[2] * keep_x
    weight_zdown = jnp.pad(weight_zup, ((1, 0), (0, 0), (0, 0)))[:-1]
    weight_ydown = jnp.pad(weight_yup, ((0, 0), (1, 0), (0, 0)))[:, :-1]
    weight_xdown = jnp.pad(weight_xup, ((0, 0), (0, 0), (1, 0)))[:, :, :-1]
    return weight_zup, weight_zdown, weight_yup, weight_ydown, weight_xup, weight_xdown


def operate(field, weights, seeded):
    weight_zup, weight_zdown, weight_yup, weight_ydown, weight_xup, weight_xdown = weights
    padded = jnp.pad(field, 1)
    laplace = weight_zup * (field - padded[2:, 1:-1, 1:-1]) + weight_zdown * (field - padded[:-2, 1:-1, 1:-1])
    laplace = laplace + weight_yup * (field - padded[1:-1, 2:, 1:-1]) + weight_ydown * (field - padded[1:-1, :-2, 1:-1])
    laplace = laplace + weight_xup * (field - padded[1:-1, 1:-1, 2:]) + weight_xdown * (field - padded[1:-1, 1:-1, :-2])
    return (1.0 - seeded) * (laplace + RIDGE_WEIGHT * field) + seeded * field


def reference(features, conv_weight, conv_bias, labels):
    affinities = affinity_head(features, conv_weight, conv_bias)
    weights = edge_weights(affinities)
    seeded = (labels > 0).astype(jnp.float32)

    def solve_field(label_index):
        seed_field = (labels == label_index + 1).astype(jnp.float32)
        right_side = seed_field - operate(seed_field, weights, seeded)
        solution = jnp.zeros_like(right_side)
        residual = right_side
        direction = right_side
        norm_now = jnp.sum(residual * residual)
        for iteration in range(ITERS):
            applied = operate(direction, weights, seeded)
            step_size = norm_now / jnp.sum(direction * applied)
            solution = solution + step_size * direction
            residual = residual - step_size * applied
            norm_next = jnp.sum(residual * residual)
            direction = residual + (norm_next / norm_now) * direction
            norm_now = norm_next
        return seed_field + solution

    probabilities = lax.map(solve_field, jnp.arange(FIELDS, dtype=jnp.int32))
    return probabilities, affinities
```

```python
import jax
import jax.numpy as jnp
from jax import lax
from jax.sharding import PartitionSpec as P

FIELDS = 8
ITERS = 3


RIDGE_WEIGHT = 0.5


def padded_2(cells, sides, width):
    for axis, dim in sides:
        count = lax.axis_size(axis)
        ends = count - 1
        head = lax.slice_in_dim(cells, 0, width, axis=dim)
        tail = lax.slice_in_dim(cells, cells.shape[dim] - width, cells.shape[dim], axis=dim)
        cells = jnp.concatenate(
            [
                lax.ppermute(tail, axis, [(i, (i + 1) % count) for i in range(ends)]),
                cells,
                lax.ppermute(head, axis, [((i + 1) % count, i) for i in range(ends)]),
            ],
            axis=dim,
        )
    return cells


def from_behind(value, axis, by):
    devices = lax.axis_size(axis)
    pairs = [(i, i + by) for i in range(devices) if 0 <= i + by < devices]
    return lax.ppermute(value, axis, pairs)


def conv_region(padded, conv_weight, count_z, count_y):
    col_cells = padded.shape[3] - 2
    summed = jnp.zeros((3, count_z, count_y, col_cells), jnp.float32)
    for offset_z in range(3):
        for offset_y in range(3):
            for offset_x in range(3):
                window = padded[
                    :,
                    offset_z : offset_z + count_z,
                    offset_y : offset_y + count_y,
                    offset_x : offset_x + col_cells,
                ]
                summed = summed + jnp.einsum(
                    "oc,czyx->ozyx",
                    conv_weight[:, :, offset_z, offset_y, offset_x],
                    window,
                    preferred_element_type=jnp.float32,
                )
    return summed


def neighbours(field):
    below_z = from_behind(field[:, -1], "gz", 1)
    above_z = from_behind(field[:, 0], "gz", -1)
    below_y = from_behind(field[:, :, -1], "yx", 1)
    above_y = from_behind(field[:, :, 0], "yx", -1)
    up_z = jnp.concatenate([field[:, 1:], above_z[:, None]], axis=1)
    down_z = jnp.concatenate([below_z[:, None], field[:, :-1]], axis=1)
    up_y = jnp.concatenate([field[:, :, 1:], above_y[:, :, None]], axis=2)
    down_y = jnp.concatenate([below_y[:, :, None], field[:, :, :-1]], axis=2)
    zero_col = jnp.zeros_like(field[..., :1])
    up_x = jnp.concatenate([field[..., 1:], zero_col], axis=3)
    down_x = jnp.concatenate([zero_col, field[..., :-1]], axis=3)
    return up_z, down_z, up_y, down_y, up_x, down_x


def operate(field, weights, seeded):
    weight_zup, weight_zdown, weight_yup, weight_ydown, weight_xup, weight_xdown = weights
    up_z, down_z, up_y, down_y, up_x, down_x = neighbours(field)
    laplace = weight_zup * (field - up_z) + weight_zdown * (field - down_z)
    laplace = laplace + weight_yup * (field - up_y) + weight_ydown * (field - down_y)
    laplace = laplace + weight_xup * (field - up_x) + weight_xdown * (field - down_x)
    return (1.0 - seeded) * (laplace + RIDGE_WEIGHT * field) + seeded * field


def field_sums(left, right):
    return jnp.sum(left * right, axis=(1, 2, 3))


def body(features, conv_weight, conv_bias, labels):
    depth_cells = features.shape[1]
    row_cells = features.shape[2]
    col_cells = features.shape[3]
    global_z = lax.axis_index("gz") * depth_cells + jnp.arange(depth_cells, dtype=jnp.int32)
    global_y = lax.axis_index("yx") * row_cells + jnp.arange(row_cells, dtype=jnp.int32)
    keep_z = (global_z < depth_cells * lax.axis_size("gz") - 1).astype(jnp.float32)[:, None, None]
    keep_y = (global_y < row_cells * lax.axis_size("yx") - 1).astype(jnp.float32)[None, :, None]
    keep_x = (jnp.arange(col_cells, dtype=jnp.int32) < col_cells - 1).astype(jnp.float32)[
        None, None, :
    ]
    bias_column = conv_bias[:, None, None, None]
    padded = padded_2(features, (("gz", 1), ("yx", 2)), 1)
    padded = jnp.pad(padded, ((0, 0), (0, 0), (0, 0), (1, 1)))
    affinities = jax.nn.sigmoid(
        conv_region(padded, conv_weight, depth_cells, row_cells) + bias_column
    )
    below_plane = from_behind(affinities[0, -1], "gz", 1)
    below_row = from_behind(affinities[1, :, -1], "yx", 1)
    weight_zdown = jnp.concatenate([below_plane[None], affinities[0, :-1]], axis=0)
    weight_ydown = jnp.concatenate([below_row[:, None, :], affinities[1, :, :-1]], axis=1)
    weight_zup = affinities[0] * keep_z
    weight_yup = affinities[1] * keep_y
    weight_xup = affinities[2] * keep_x
    weight_xdown = jnp.pad(weight_xup, ((0, 0), (0, 0), (1, 0)))[:, :, :-1]
    weights = (
        weight_zup[None],
        weight_zdown[None],
        weight_yup[None],
        weight_ydown[None],
        weight_xup[None],
        weight_xdown[None],
    )
    seeded = (labels > 0).astype(jnp.float32)[None]
    colours = jnp.arange(1, FIELDS + 1, dtype=jnp.int32)[:, None, None, None]
    seed_field = (labels[None] == colours).astype(jnp.float32)

    basis = [seed_field - operate(seed_field, weights, seeded)]
    for power in range(ITERS):
        basis.append(operate(basis[-1], weights, seeded))
    size = ITERS + 1
    pairs = [(i, j) for i in range(size) for j in range(i, size) if i < size - 1]
    local = jnp.stack([field_sums(basis[i], basis[j]) for i, j in pairs])
    total = lax.psum(local, ("gz", "yx"))
    gram = {}
    for index, (i, j) in enumerate(pairs):
        gram[i, j] = total[index]
        gram[j, i] = total[index]

    zero = jnp.zeros((FIELDS,), jnp.float32)
    one = jnp.ones((FIELDS,), jnp.float32)

    def inner(left, right):
        acc = zero
        for i in range(size):
            for j in range(size):
                if (i, j) in gram and not (
                    isinstance(left[i], float) or isinstance(right[j], float)
                ):
                    acc = acc + left[i] * gram[i, j] * right[j]
        return acc

    def shift(coeffs):
        return [0.0] + coeffs[:-1]

    def axpy(scale, left, right):
        out = []
        for a, b in zip(left, right):
            if isinstance(b, float):
                out.append(a)
            elif isinstance(a, float):
                out.append(scale * b)
            else:
                out.append(a + scale * b)
        return out

    residual = [one] + [0.0] * (size - 1)
    direction = list(residual)
    solution = [0.0] * size
    norm_now = inner(residual, residual)
    for iteration in range(ITERS):
        applied = shift(direction)
        step_size = norm_now / inner(direction, applied)
        solution = axpy(step_size, solution, direction)
        if iteration == ITERS - 1:
            break
        residual = axpy(-step_size, residual, applied)
        norm_next = inner(residual, residual)
        direction = axpy(norm_next / norm_now, residual, direction)
        norm_now = norm_next

    probabilities = seed_field
    for coeff, vector in zip(solution, basis):
        if not isinstance(coeff, float):
            probabilities = probabilities + coeff[:, None, None, None] * vector
    return (probabilities, affinities)


def solution(mesh):
    in_specs = (P(None, "gz", "yx", None), P(), P(), P("gz", "yx", None))
    out_specs = (P(None, "gz", "yx", None), P(None, "gz", "yx", None))
    return jax.shard_map(body, mesh=mesh, in_specs=in_specs, out_specs=out_specs, check_vma=False)
```

```python
import jax
import jax.numpy as jnp
from jax import lax
from jax.sharding import PartitionSpec as P

FIELDS = 8
ITERS = 3


RIDGE_WEIGHT = 0.5


def padded_2(cells, sides, width):
    for axis, dim in sides:
        count = lax.axis_size(axis)
        ends = count - 1
        head = lax.slice_in_dim(cells, 0, width, axis=dim)
        tail = lax.slice_in_dim(cells, cells.shape[dim] - width, cells.shape[dim], axis=dim)
        cells = jnp.concatenate(
            [
                lax.ppermute(tail, axis, [(i, (i + 1) % count) for i in range(ends)]),
                cells,
                lax.ppermute(head, axis, [((i + 1) % count, i) for i in range(ends)]),
            ],
            axis=dim,
        )
    return cells


def from_behind(value, axis, by):
    devices = lax.axis_size(axis)
    pairs = [(i, i + by) for i in range(devices) if 0 <= i + by < devices]
    return lax.ppermute(value, axis, pairs)


def conv_region(padded, conv_weight, count_z, count_y):
    col_cells = padded.shape[3] - 2
    summed = jnp.zeros((3, count_z, count_y, col_cells), jnp.float32)
    for offset_z in range(3):
        for offset_y in range(3):
            for offset_x in range(3):
                window = padded[
                    :,
                    offset_z : offset_z + count_z,
                    offset_y : offset_y + count_y,
                    offset_x : offset_x + col_cells,
                ]
                summed = summed + jnp.einsum(
                    "oc,czyx->ozyx",
                    conv_weight[:, :, offset_z, offset_y, offset_x],
                    window,
                    preferred_element_type=jnp.float32,
                )
    return summed


def neighbours(field):
    below_z = from_behind(field[:, -1], "gz", 1)
    above_z = from_behind(field[:, 0], "gz", -1)
    below_y = from_behind(field[:, :, -1], "yx", 1)
    above_y = from_behind(field[:, :, 0], "yx", -1)
    up_z = jnp.concatenate([field[:, 1:], above_z[:, None]], axis=1)
    down_z = jnp.concatenate([below_z[:, None], field[:, :-1]], axis=1)
    up_y = jnp.concatenate([field[:, :, 1:], above_y[:, :, None]], axis=2)
    down_y = jnp.concatenate([below_y[:, :, None], field[:, :, :-1]], axis=2)
    zero_col = jnp.zeros_like(field[..., :1])
    up_x = jnp.concatenate([field[..., 1:], zero_col], axis=3)
    down_x = jnp.concatenate([zero_col, field[..., :-1]], axis=3)
    return up_z, down_z, up_y, down_y, up_x, down_x


def operate(field, weights, seeded):
    weight_zup, weight_zdown, weight_yup, weight_ydown, weight_xup, weight_xdown = weights
    up_z, down_z, up_y, down_y, up_x, down_x = neighbours(field)
    laplace = weight_zup * (field - up_z) + weight_zdown * (field - down_z)
    laplace = laplace + weight_yup * (field - up_y) + weight_ydown * (field - down_y)
    laplace = laplace + weight_xup * (field - up_x) + weight_xdown * (field - down_x)
    return (1.0 - seeded) * (laplace + RIDGE_WEIGHT * field) + seeded * field


def all_sum(value, axes):
    for axis in axes:
        devices = lax.axis_size(axis)
        if devices & (devices - 1):
            value = lax.psum(value, axis)
            continue
        hop = 1
        while hop < devices:
            value = value + lax.ppermute(value, axis, [(i, i ^ hop) for i in range(devices)])
            hop *= 2
    return value


def field_sums(left, right):
    return jnp.sum(left * right, axis=(1, 2, 3))


def body(features, conv_weight, conv_bias, labels):
    depth_cells = features.shape[1]
    row_cells = features.shape[2]
    col_cells = features.shape[3]
    global_z = lax.axis_index("gz") * depth_cells + jnp.arange(depth_cells, dtype=jnp.int32)
    global_y = lax.axis_index("yx") * row_cells + jnp.arange(row_cells, dtype=jnp.int32)
    keep_z = (global_z < depth_cells * lax.axis_size("gz") - 1).astype(jnp.float32)[:, None, None]
    keep_y = (global_y < row_cells * lax.axis_size("yx") - 1).astype(jnp.float32)[None, :, None]
    keep_x = (jnp.arange(col_cells, dtype=jnp.int32) < col_cells - 1).astype(jnp.float32)[
        None, None, :
    ]
    bias_column = conv_bias[:, None, None, None]
    padded = padded_2(features, (("gz", 1), ("yx", 2)), 1)
    padded = jnp.pad(padded, ((0, 0), (0, 0), (0, 0), (1, 1)))
    affinities = jax.nn.sigmoid(
        conv_region(padded, conv_weight, depth_cells, row_cells) + bias_column
    )
    below_plane = from_behind(affinities[0, -1], "gz", 1)
    below_row = from_behind(affinities[1, :, -1], "yx", 1)
    weight_zdown = jnp.concatenate([below_plane[None], affinities[0, :-1]], axis=0)
    weight_ydown = jnp.concatenate([below_row[:, None, :], affinities[1, :, :-1]], axis=1)
    weight_zup = affinities[0] * keep_z
    weight_yup = affinities[1] * keep_y
    weight_xup = affinities[2] * keep_x
    weight_xdown = jnp.pad(weight_xup, ((0, 0), (0, 0), (1, 0)))[:, :, :-1]
    weights = (
        weight_zup[None],
        weight_zdown[None],
        weight_yup[None],
        weight_ydown[None],
        weight_xup[None],
        weight_xdown[None],
    )
    seeded = (labels > 0).astype(jnp.float32)[None]
    colours = jnp.arange(1, FIELDS + 1, dtype=jnp.int32)[:, None, None, None]
    seed_field = (labels[None] == colours).astype(jnp.float32)

    basis = [seed_field - operate(seed_field, weights, seeded)]
    for power in range(ITERS):
        basis.append(operate(basis[-1], weights, seeded))
    size = ITERS + 1
    pairs = [(i, j) for i in range(size) for j in range(i, size) if i < size - 1]
    local = jnp.stack([field_sums(basis[i], basis[j]) for i, j in pairs])
    total = all_sum(local, ("gz", "yx"))
    gram = {}
    for index, (i, j) in enumerate(pairs):
        gram[i, j] = total[index]
        gram[j, i] = total[index]

    zero = jnp.zeros((FIELDS,), jnp.float32)
    one = jnp.ones((FIELDS,), jnp.float32)

    def inner(left, right):
        acc = zero
        for i in range(size):
            for j in range(size):
                if (i, j) in gram and not (
                    isinstance(left[i], float) or isinstance(right[j], float)
                ):
                    acc = acc + left[i] * gram[i, j] * right[j]
        return acc

    def shift(coeffs):
        return [0.0] + coeffs[:-1]

    def axpy(scale, left, right):
        out = []
        for a, b in zip(left, right):
            if isinstance(b, float):
                out.append(a)
            elif isinstance(a, float):
                out.append(scale * b)
            else:
                out.append(a + scale * b)
        return out

    residual = [one] + [0.0] * (size - 1)
    direction = list(residual)
    solution = [0.0] * size
    norm_now = inner(residual, residual)
    for iteration in range(ITERS):
        applied = shift(direction)
        step_size = norm_now / inner(direction, applied)
        solution = axpy(step_size, solution, direction)
        if iteration == ITERS - 1:
            break
        residual = axpy(-step_size, residual, applied)
        norm_next = inner(residual, residual)
        direction = axpy(norm_next / norm_now, residual, direction)
        norm_now = norm_next

    probabilities = seed_field
    for coeff, vector in zip(solution, basis):
        if not isinstance(coeff, float):
            probabilities = probabilities + coeff[:, None, None, None] * vector
    return (probabilities, affinities)


def solution(mesh):
    in_specs = (P(None, "gz", "yx", None), P(), P(), P("gz", "yx", None))
    out_specs = (P(None, "gz", "yx", None), P(None, "gz", "yx", None))
    return jax.shard_map(body, mesh=mesh, in_specs=in_specs, out_specs=out_specs, check_vma=False)
```

```python
import jax
import jax.numpy as jnp
from jax import lax
from jax.sharding import PartitionSpec as P

FIELDS = 8
ITERS = 3


RIDGE_WEIGHT = 0.5


def padded_2(cells, sides, width):
    for axis, dim in sides:
        count = lax.axis_size(axis)
        ends = count - 1
        head = lax.slice_in_dim(cells, 0, width, axis=dim)
        tail = lax.slice_in_dim(cells, cells.shape[dim] - width, cells.shape[dim], axis=dim)
        cells = jnp.concatenate(
            [
                lax.ppermute(tail, axis, [(i, (i + 1) % count) for i in range(ends)]),
                cells,
                lax.ppermute(head, axis, [((i + 1) % count, i) for i in range(ends)]),
            ],
            axis=dim,
        )
    return cells


def from_behind(value, axis, by):
    devices = lax.axis_size(axis)
    pairs = [(i, i + by) for i in range(devices) if 0 <= i + by < devices]
    return lax.ppermute(value, axis, pairs)


def conv_region(padded, conv_weight, count_z, count_y):
    col_cells = padded.shape[3] - 2
    summed = jnp.zeros((3, count_z, count_y, col_cells), jnp.float32)
    for offset_z in range(3):
        for offset_y in range(3):
            for offset_x in range(3):
                window = padded[
                    :,
                    offset_z : offset_z + count_z,
                    offset_y : offset_y + count_y,
                    offset_x : offset_x + col_cells,
                ]
                summed = summed + jnp.einsum(
                    "oc,czyx->ozyx",
                    conv_weight[:, :, offset_z, offset_y, offset_x],
                    window,
                    preferred_element_type=jnp.float32,
                )
    return summed


def extend(cells, width):
    for axis, dim in (("gz", 1), ("yx", 2)):
        size = cells.shape[dim]
        head = lax.slice_in_dim(cells, 0, width, axis=dim)
        tail = lax.slice_in_dim(cells, size - width, size, axis=dim)
        cells = jnp.concatenate(
            [from_behind(tail, axis, 1), cells, from_behind(head, axis, -1)], axis=dim
        )
    return cells


def operate_inside(field, grid, offset):
    weight_zup, weight_yup, weight_x, seeded = grid
    count = field.shape[1] - 2
    inner = slice(offset, offset + count)
    lower = slice(offset - 1, offset - 1 + count)
    centre = field[:, 1:-1, 1:-1]
    weight_xup = weight_x[inner, inner]
    weight_xdown = jnp.pad(weight_xup, ((0, 0), (0, 0), (1, 0)))[:, :, :-1]
    zero_col = jnp.zeros_like(centre[..., :1])
    laplace = weight_zup[inner, inner] * (centre - field[:, 2:, 1:-1]) + weight_zup[lower, inner] * (
        centre - field[:, :-2, 1:-1]
    )
    laplace = (
        laplace
        + weight_yup[inner, inner] * (centre - field[:, 1:-1, 2:])
        + weight_yup[inner, lower] * (centre - field[:, 1:-1, :-2])
    )
    laplace = (
        laplace
        + weight_xup * (centre - jnp.concatenate([centre[..., 1:], zero_col], axis=3))
        + weight_xdown * (centre - jnp.concatenate([zero_col, centre[..., :-1]], axis=3))
    )
    mask = seeded[inner, inner]
    return (1.0 - mask) * (laplace + RIDGE_WEIGHT * centre) + mask * centre


def all_sum(value, axes):
    for axis in axes:
        devices = lax.axis_size(axis)
        if devices & (devices - 1):
            value = lax.psum(value, axis)
            continue
        hop = 1
        while hop < devices:
            value = value + lax.ppermute(value, axis, [(i, i ^ hop) for i in range(devices)])
            hop *= 2
    return value


def field_sums(left, right):
    return jnp.sum(left * right, axis=(1, 2, 3))


def body(features, conv_weight, conv_bias, labels):
    depth_cells = features.shape[1]
    row_cells = features.shape[2]
    col_cells = features.shape[3]
    global_z = lax.axis_index("gz") * depth_cells + jnp.arange(depth_cells, dtype=jnp.int32)
    global_y = lax.axis_index("yx") * row_cells + jnp.arange(row_cells, dtype=jnp.int32)
    keep_z = (global_z < depth_cells * lax.axis_size("gz") - 1).astype(jnp.float32)[:, None, None]
    keep_y = (global_y < row_cells * lax.axis_size("yx") - 1).astype(jnp.float32)[None, :, None]
    keep_x = (jnp.arange(col_cells, dtype=jnp.int32) < col_cells - 1).astype(jnp.float32)[
        None, None, :
    ]
    bias_column = conv_bias[:, None, None, None]
    padded = padded_2(features, (("gz", 1), ("yx", 2)), 1)
    padded = jnp.pad(padded, ((0, 0), (0, 0), (0, 0), (1, 1)))
    affinities = jax.nn.sigmoid(
        conv_region(padded, conv_weight, depth_cells, row_cells) + bias_column
    )
    halo = ITERS + 1
    stacked = jnp.concatenate([affinities, labels[None].astype(jnp.float32)], axis=0)
    grid_cells = extend(stacked, halo)
    cells_z = depth_cells + 2 * halo
    cells_y = row_cells + 2 * halo
    grid_z = lax.axis_index("gz") * depth_cells - halo + jnp.arange(cells_z, dtype=jnp.int32)
    grid_y = lax.axis_index("yx") * row_cells - halo + jnp.arange(cells_y, dtype=jnp.int32)
    edge_z = ((grid_z >= 0) & (grid_z < depth_cells * lax.axis_size("gz") - 1)).astype(jnp.float32)
    edge_y = ((grid_y >= 0) & (grid_y < row_cells * lax.axis_size("yx") - 1)).astype(jnp.float32)
    grid_labels = grid_cells[3]
    grid = (
        grid_cells[0] * edge_z[:, None, None],
        grid_cells[1] * edge_y[None, :, None],
        grid_cells[2] * keep_x,
        (grid_labels > 0.5).astype(jnp.float32),
    )
    colours = jnp.arange(1, FIELDS + 1, dtype=jnp.float32)[:, None, None, None]
    grid_seed = (grid_labels[None] == colours).astype(jnp.float32)
    seed_field = grid_seed[:, halo:-halo, halo:-halo]

    inside = grid_seed[:, 1:-1, 1:-1]
    current = inside - operate_inside(grid_seed, grid, 1)
    basis = [current]
    for power in range(ITERS):
        current = operate_inside(current, grid, power + 2)
        basis.append(current)
    basis = [
        vector[:, (vector.shape[1] - depth_cells) // 2 : (vector.shape[1] + depth_cells) // 2,
               (vector.shape[2] - row_cells) // 2 : (vector.shape[2] + row_cells) // 2]
        for vector in basis
    ]
    size = ITERS + 1
    pairs = [(i, j) for i in range(size) for j in range(i, size) if i < size - 1]
    local = jnp.stack([field_sums(basis[i], basis[j]) for i, j in pairs])
    total = all_sum(local, ("gz", "yx"))
    gram = {}
    for index, (i, j) in enumerate(pairs):
        gram[i, j] = total[index]
        gram[j, i] = total[index]

    zero = jnp.zeros((FIELDS,), jnp.float32)
    one = jnp.ones((FIELDS,), jnp.float32)

    def inner(left, right):
        acc = zero
        for i in range(size):
            for j in range(size):
                if (i, j) in gram and not (
                    isinstance(left[i], float) or isinstance(right[j], float)
                ):
                    acc = acc + left[i] * gram[i, j] * right[j]
        return acc

    def shift(coeffs):
        return [0.0] + coeffs[:-1]

    def axpy(scale, left, right):
        out = []
        for a, b in zip(left, right):
            if isinstance(b, float):
                out.append(a)
            elif isinstance(a, float):
                out.append(scale * b)
            else:
                out.append(a + scale * b)
        return out

    residual = [one] + [0.0] * (size - 1)
    direction = list(residual)
    solution = [0.0] * size
    norm_now = inner(residual, residual)
    for iteration in range(ITERS):
        applied = shift(direction)
        step_size = norm_now / inner(direction, applied)
        solution = axpy(step_size, solution, direction)
        if iteration == ITERS - 1:
            break
        residual = axpy(-step_size, residual, applied)
        norm_next = inner(residual, residual)
        direction = axpy(norm_next / norm_now, residual, direction)
        norm_now = norm_next

    probabilities = seed_field
    for coeff, vector in zip(solution, basis):
        if not isinstance(coeff, float):
            probabilities = probabilities + coeff[:, None, None, None] * vector
    return (probabilities, affinities)


def solution(mesh):
    in_specs = (P(None, "gz", "yx", None), P(), P(), P("gz", "yx", None))
    out_specs = (P(None, "gz", "yx", None), P(None, "gz", "yx", None))
    return jax.shard_map(body, mesh=mesh, in_specs=in_specs, out_specs=out_specs, check_vma=False)
```

```python
import jax
import jax.numpy as jnp
from jax import lax
from jax.sharding import PartitionSpec as P

FIELDS = 8
ITERS = 3


RIDGE_WEIGHT = 0.5


def padded_2(cells, sides, width):
    for axis, dim in sides:
        count = lax.axis_size(axis)
        ends = count - 1
        head = lax.slice_in_dim(cells, 0, width, axis=dim)
        tail = lax.slice_in_dim(cells, cells.shape[dim] - width, cells.shape[dim], axis=dim)
        cells = jnp.concatenate(
            [
                lax.ppermute(tail, axis, [(i, (i + 1) % count) for i in range(ends)]),
                cells,
                lax.ppermute(head, axis, [((i + 1) % count, i) for i in range(ends)]),
            ],
            axis=dim,
        )
    return cells


def from_behind(value, axis, by):
    devices = lax.axis_size(axis)
    pairs = [(i, i + by) for i in range(devices) if 0 <= i + by < devices]
    return lax.ppermute(value, axis, pairs)


def conv_region(padded, conv_weight, count_z, count_y):
    col_cells = padded.shape[3] - 2
    summed = jnp.zeros((3, count_z, count_y, col_cells), jnp.float32)
    for offset_z in range(3):
        for offset_y in range(3):
            for offset_x in range(3):
                window = padded[
                    :,
                    offset_z : offset_z + count_z,
                    offset_y : offset_y + count_y,
                    offset_x : offset_x + col_cells,
                ]
                summed = summed + jnp.einsum(
                    "oc,czyx->ozyx",
                    conv_weight[:, :, offset_z, offset_y, offset_x],
                    window,
                    preferred_element_type=jnp.float32,
                )
    return summed


def extend(cells, width):
    for axis, dim in (("gz", 1), ("yx", 2)):
        size = cells.shape[dim]
        head = lax.slice_in_dim(cells, 0, width, axis=dim)
        tail = lax.slice_in_dim(cells, size - width, size, axis=dim)
        cells = jnp.concatenate(
            [from_behind(tail, axis, 1), cells, from_behind(head, axis, -1)], axis=dim
        )
    return cells


def operate_inside(field, grid, offset):
    weight_zup, weight_yup, weight_x, seeded = grid
    count = field.shape[1] - 2
    inner = slice(offset, offset + count)
    lower = slice(offset - 1, offset - 1 + count)
    centre = field[:, 1:-1, 1:-1]
    weight_xup = weight_x[inner, inner]
    weight_xdown = jnp.pad(weight_xup, ((0, 0), (0, 0), (1, 0)))[:, :, :-1]
    zero_col = jnp.zeros_like(centre[..., :1])
    laplace = weight_zup[inner, inner] * (centre - field[:, 2:, 1:-1]) + weight_zup[lower, inner] * (
        centre - field[:, :-2, 1:-1]
    )
    laplace = (
        laplace
        + weight_yup[inner, inner] * (centre - field[:, 1:-1, 2:])
        + weight_yup[inner, lower] * (centre - field[:, 1:-1, :-2])
    )
    laplace = (
        laplace
        + weight_xup * (centre - jnp.concatenate([centre[..., 1:], zero_col], axis=3))
        + weight_xdown * (centre - jnp.concatenate([zero_col, centre[..., :-1]], axis=3))
    )
    mask = seeded[inner, inner]
    return (1.0 - mask) * (laplace + RIDGE_WEIGHT * centre) + mask * centre


def all_sum(value, axes):
    for axis in axes:
        devices = lax.axis_size(axis)
        if devices & (devices - 1):
            value = lax.psum(value, axis)
            continue
        hop = 1
        while hop < devices:
            value = value + lax.ppermute(value, axis, [(i, i ^ hop) for i in range(devices)])
            hop *= 2
    return value


def field_sums(left, right):
    return jnp.sum(left * right, axis=(1, 2, 3))


def body(features, conv_weight, conv_bias, labels):
    depth_cells = features.shape[1]
    row_cells = features.shape[2]
    col_cells = features.shape[3]
    global_z = lax.axis_index("gz") * depth_cells + jnp.arange(depth_cells, dtype=jnp.int32)
    global_y = lax.axis_index("yx") * row_cells + jnp.arange(row_cells, dtype=jnp.int32)
    keep_z = (global_z < depth_cells * lax.axis_size("gz") - 1).astype(jnp.float32)[:, None, None]
    keep_y = (global_y < row_cells * lax.axis_size("yx") - 1).astype(jnp.float32)[None, :, None]
    keep_x = (jnp.arange(col_cells, dtype=jnp.int32) < col_cells - 1).astype(jnp.float32)[
        None, None, :
    ]
    halo = ITERS + 1
    stacked = jnp.concatenate([features, labels[None].astype(features.dtype)], axis=0)
    grid_cells = extend(stacked, halo + 1)
    channels = features.shape[0]
    response = lax.conv_general_dilated(
        grid_cells[None, :channels],
        conv_weight,
        window_strides=(1, 1, 1),
        padding=((0, 0), (0, 0), (1, 1)),
        dimension_numbers=("NCDHW", "OIDHW", "NCDHW"),
        preferred_element_type=jnp.float32,
    )[0]
    grid_aff = jax.nn.sigmoid(response + conv_bias[:, None, None, None])
    affinities = grid_aff[:, halo:-halo, halo:-halo]
    grid_labels = grid_cells[channels, 1:-1, 1:-1].astype(jnp.float32)
    cells_z = depth_cells + 2 * halo
    cells_y = row_cells + 2 * halo
    grid_z = lax.axis_index("gz") * depth_cells - halo + jnp.arange(cells_z, dtype=jnp.int32)
    grid_y = lax.axis_index("yx") * row_cells - halo + jnp.arange(cells_y, dtype=jnp.int32)
    edge_z = ((grid_z >= 0) & (grid_z < depth_cells * lax.axis_size("gz") - 1)).astype(jnp.float32)
    edge_y = ((grid_y >= 0) & (grid_y < row_cells * lax.axis_size("yx") - 1)).astype(jnp.float32)
    grid = (
        grid_aff[0] * edge_z[:, None, None],
        grid_aff[1] * edge_y[None, :, None],
        grid_aff[2] * keep_x,
        (grid_labels > 0.5).astype(jnp.float32),
    )
    colours = jnp.arange(1, FIELDS + 1, dtype=jnp.float32)[:, None, None, None]
    grid_seed = (grid_labels[None] == colours).astype(jnp.float32)
    seed_field = grid_seed[:, halo:-halo, halo:-halo]

    inside = grid_seed[:, 1:-1, 1:-1]
    current = inside - operate_inside(grid_seed, grid, 1)
    basis = [current]
    for power in range(ITERS):
        current = operate_inside(current, grid, power + 2)
        basis.append(current)
    basis = [
        vector[:, (vector.shape[1] - depth_cells) // 2 : (vector.shape[1] + depth_cells) // 2,
               (vector.shape[2] - row_cells) // 2 : (vector.shape[2] + row_cells) // 2]
        for vector in basis
    ]
    size = ITERS + 1
    pairs = [(i, j) for i in range(size) for j in range(i, size) if i < size - 1]
    local = jnp.stack([field_sums(basis[i], basis[j]) for i, j in pairs])
    total = all_sum(local, ("gz", "yx"))
    gram = {}
    for index, (i, j) in enumerate(pairs):
        gram[i, j] = total[index]
        gram[j, i] = total[index]

    zero = jnp.zeros((FIELDS,), jnp.float32)
    one = jnp.ones((FIELDS,), jnp.float32)

    def inner(left, right):
        acc = zero
        for i in range(size):
            for j in range(size):
                if (i, j) in gram and not (
                    isinstance(left[i], float) or isinstance(right[j], float)
                ):
                    acc = acc + left[i] * gram[i, j] * right[j]
        return acc

    def shift(coeffs):
        return [0.0] + coeffs[:-1]

    def axpy(scale, left, right):
        out = []
        for a, b in zip(left, right):
            if isinstance(b, float):
                out.append(a)
            elif isinstance(a, float):
                out.append(scale * b)
            else:
                out.append(a + scale * b)
        return out

    residual = [one] + [0.0] * (size - 1)
    direction = list(residual)
    solution = [0.0] * size
    norm_now = inner(residual, residual)
    for iteration in range(ITERS):
        applied = shift(direction)
        step_size = norm_now / inner(direction, applied)
        solution = axpy(step_size, solution, direction)
        if iteration == ITERS - 1:
            break
        residual = axpy(-step_size, residual, applied)
        norm_next = inner(residual, residual)
        direction = axpy(norm_next / norm_now, residual, direction)
        norm_now = norm_next

    probabilities = seed_field
    for coeff, vector in zip(solution, basis):
        if not isinstance(coeff, float):
            probabilities = probabilities + coeff[:, None, None, None] * vector
    return (probabilities, affinities)


def solution(mesh):
    in_specs = (P(None, "gz", "yx", None), P(), P(), P("gz", "yx", None))
    out_specs = (P(None, "gz", "yx", None), P(None, "gz", "yx", None))
    return jax.shard_map(body, mesh=mesh, in_specs=in_specs, out_specs=out_specs, check_vma=False)
```

```python
import jax
import jax.numpy as jnp
from jax import lax
from jax.sharding import PartitionSpec as P

FIELDS = 8
ITERS = 3


RIDGE_WEIGHT = 0.5


def padded_2(cells, sides, width):
    for axis, dim in sides:
        count = lax.axis_size(axis)
        ends = count - 1
        head = lax.slice_in_dim(cells, 0, width, axis=dim)
        tail = lax.slice_in_dim(cells, cells.shape[dim] - width, cells.shape[dim], axis=dim)
        cells = jnp.concatenate(
            [
                lax.ppermute(tail, axis, [(i, (i + 1) % count) for i in range(ends)]),
                cells,
                lax.ppermute(head, axis, [((i + 1) % count, i) for i in range(ends)]),
            ],
            axis=dim,
        )
    return cells


def from_behind(value, axis, by):
    devices = lax.axis_size(axis)
    pairs = [(i, i + by) for i in range(devices) if 0 <= i + by < devices]
    return lax.ppermute(value, axis, pairs)


def conv_region(padded, conv_weight, count_z, count_y):
    col_cells = padded.shape[3] - 2
    shifted = jnp.stack(
        [padded[..., offset_x : offset_x + col_cells] for offset_x in range(3)], axis=1
    )
    summed = jnp.zeros((3, count_z, count_y, col_cells), jnp.float32)
    for offset_z in range(3):
        for offset_y in range(3):
            window = shifted[
                :, :, offset_z : offset_z + count_z, offset_y : offset_y + count_y
            ]
            summed = summed + jnp.einsum(
                "oce,cezyx->ozyx",
                conv_weight[:, :, offset_z, offset_y, :],
                window,
                preferred_element_type=jnp.float32,
            )
    return summed


def extend(cells, width):
    for axis, dim in (("gz", 1), ("yx", 2)):
        size = cells.shape[dim]
        head = lax.slice_in_dim(cells, 0, width, axis=dim)
        tail = lax.slice_in_dim(cells, size - width, size, axis=dim)
        cells = jnp.concatenate(
            [from_behind(tail, axis, 1), cells, from_behind(head, axis, -1)], axis=dim
        )
    return cells


def operate_inside(field, grid, offset):
    weight_zup, weight_yup, weight_x, seeded = grid
    count = field.shape[1] - 2
    inner = slice(offset, offset + count)
    lower = slice(offset - 1, offset - 1 + count)
    centre = field[:, 1:-1, 1:-1]
    weight_xup = weight_x[inner, inner]
    weight_xdown = jnp.pad(weight_xup, ((0, 0), (0, 0), (1, 0)))[:, :, :-1]
    zero_col = jnp.zeros_like(centre[..., :1])
    laplace = weight_zup[inner, inner] * (centre - field[:, 2:, 1:-1]) + weight_zup[lower, inner] * (
        centre - field[:, :-2, 1:-1]
    )
    laplace = (
        laplace
        + weight_yup[inner, inner] * (centre - field[:, 1:-1, 2:])
        + weight_yup[inner, lower] * (centre - field[:, 1:-1, :-2])
    )
    laplace = (
        laplace
        + weight_xup * (centre - jnp.concatenate([centre[..., 1:], zero_col], axis=3))
        + weight_xdown * (centre - jnp.concatenate([zero_col, centre[..., :-1]], axis=3))
    )
    mask = seeded[inner, inner]
    return (1.0 - mask) * (laplace + RIDGE_WEIGHT * centre) + mask * centre


def all_sum(value, axes):
    for axis in axes:
        devices = lax.axis_size(axis)
        if devices & (devices - 1):
            value = lax.psum(value, axis)
            continue
        hop = 1
        while hop < devices:
            value = value + lax.ppermute(value, axis, [(i, i ^ hop) for i in range(devices)])
            hop *= 2
    return value


def field_sums(left, right):
    return jnp.sum(left * right, axis=(1, 2, 3))


def body(features, conv_weight, conv_bias, labels):
    depth_cells = features.shape[1]
    row_cells = features.shape[2]
    col_cells = features.shape[3]
    global_z = lax.axis_index("gz") * depth_cells + jnp.arange(depth_cells, dtype=jnp.int32)
    global_y = lax.axis_index("yx") * row_cells + jnp.arange(row_cells, dtype=jnp.int32)
    keep_z = (global_z < depth_cells * lax.axis_size("gz") - 1).astype(jnp.float32)[:, None, None]
    keep_y = (global_y < row_cells * lax.axis_size("yx") - 1).astype(jnp.float32)[None, :, None]
    keep_x = (jnp.arange(col_cells, dtype=jnp.int32) < col_cells - 1).astype(jnp.float32)[
        None, None, :
    ]
    bias_column = conv_bias[:, None, None, None]
    padded = padded_2(features, (("gz", 1), ("yx", 2)), 1)
    padded = jnp.pad(padded, ((0, 0), (0, 0), (0, 0), (1, 1)))
    affinities = jax.nn.sigmoid(
        conv_region(padded, conv_weight, depth_cells, row_cells) + bias_column
    )
    halo = ITERS + 1
    stacked = jnp.concatenate([affinities, labels[None].astype(jnp.float32)], axis=0)
    grid_cells = extend(stacked, halo)
    cells_z = depth_cells + 2 * halo
    cells_y = row_cells + 2 * halo
    grid_z = lax.axis_index("gz") * depth_cells - halo + jnp.arange(cells_z, dtype=jnp.int32)
    grid_y = lax.axis_index("yx") * row_cells - halo + jnp.arange(cells_y, dtype=jnp.int32)
    edge_z = ((grid_z >= 0) & (grid_z < depth_cells * lax.axis_size("gz") - 1)).astype(jnp.float32)
    edge_y = ((grid_y >= 0) & (grid_y < row_cells * lax.axis_size("yx") - 1)).astype(jnp.float32)
    grid_labels = grid_cells[3]
    grid = (
        grid_cells[0] * edge_z[:, None, None],
        grid_cells[1] * edge_y[None, :, None],
        grid_cells[2] * keep_x,
        (grid_labels > 0.5).astype(jnp.float32),
    )
    colours = jnp.arange(1, FIELDS + 1, dtype=jnp.float32)[:, None, None, None]
    grid_seed = (grid_labels[None] == colours).astype(jnp.float32)
    seed_field = grid_seed[:, halo:-halo, halo:-halo]

    inside = grid_seed[:, 1:-1, 1:-1]
    current = inside - operate_inside(grid_seed, grid, 1)
    basis = [current]
    for power in range(ITERS):
        current = operate_inside(current, grid, power + 2)
        basis.append(current)
    basis = [
        vector[:, (vector.shape[1] - depth_cells) // 2 : (vector.shape[1] + depth_cells) // 2,
               (vector.shape[2] - row_cells) // 2 : (vector.shape[2] + row_cells) // 2]
        for vector in basis
    ]
    size = ITERS + 1
    pairs = [(i, j) for i in range(size) for j in range(i, size) if i < size - 1]
    local = jnp.stack([field_sums(basis[i], basis[j]) for i, j in pairs])
    total = all_sum(local, ("gz", "yx"))
    gram = {}
    for index, (i, j) in enumerate(pairs):
        gram[i, j] = total[index]
        gram[j, i] = total[index]

    zero = jnp.zeros((FIELDS,), jnp.float32)
    one = jnp.ones((FIELDS,), jnp.float32)

    def inner(left, right):
        acc = zero
        for i in range(size):
            for j in range(size):
                if (i, j) in gram and not (
                    isinstance(left[i], float) or isinstance(right[j], float)
                ):
                    acc = acc + left[i] * gram[i, j] * right[j]
        return acc

    def shift(coeffs):
        return [0.0] + coeffs[:-1]

    def axpy(scale, left, right):
        out = []
        for a, b in zip(left, right):
            if isinstance(b, float):
                out.append(a)
            elif isinstance(a, float):
                out.append(scale * b)
            else:
                out.append(a + scale * b)
        return out

    residual = [one] + [0.0] * (size - 1)
    direction = list(residual)
    solution = [0.0] * size
    norm_now = inner(residual, residual)
    for iteration in range(ITERS):
        applied = shift(direction)
        step_size = norm_now / inner(direction, applied)
        solution = axpy(step_size, solution, direction)
        if iteration == ITERS - 1:
            break
        residual = axpy(-step_size, residual, applied)
        norm_next = inner(residual, residual)
        direction = axpy(norm_next / norm_now, residual, direction)
        norm_now = norm_next

    probabilities = seed_field
    for coeff, vector in zip(solution, basis):
        if not isinstance(coeff, float):
            probabilities = probabilities + coeff[:, None, None, None] * vector
    return (probabilities, affinities)


def solution(mesh):
    in_specs = (P(None, "gz", "yx", None), P(), P(), P("gz", "yx", None))
    out_specs = (P(None, "gz", "yx", None), P(None, "gz", "yx", None))
    return jax.shard_map(body, mesh=mesh, in_specs=in_specs, out_specs=out_specs, check_vma=False)
```

```python
import jax
import jax.numpy as jnp
from jax import lax
from jax.sharding import PartitionSpec as P

FIELDS = 8
ITERS = 3


RIDGE_WEIGHT = 0.5


def padded_2(cells, sides, width):
    for axis, dim in sides:
        count = lax.axis_size(axis)
        ends = count - 1
        head = lax.slice_in_dim(cells, 0, width, axis=dim)
        tail = lax.slice_in_dim(cells, cells.shape[dim] - width, cells.shape[dim], axis=dim)
        cells = jnp.concatenate(
            [
                lax.ppermute(tail, axis, [(i, (i + 1) % count) for i in range(ends)]),
                cells,
                lax.ppermute(head, axis, [((i + 1) % count, i) for i in range(ends)]),
            ],
            axis=dim,
        )
    return cells


def from_behind(value, axis, by):
    devices = lax.axis_size(axis)
    pairs = [(i, i + by) for i in range(devices) if 0 <= i + by < devices]
    return lax.ppermute(value, axis, pairs)


def conv_region(padded, conv_weight, count_z, count_y):
    col_cells = padded.shape[3] - 2
    shifted = jnp.stack(
        [padded[..., offset_x : offset_x + col_cells] for offset_x in range(3)], axis=1
    )
    summed = jnp.zeros((3, count_z, count_y, col_cells), jnp.float32)
    for offset_z in range(3):
        for offset_y in range(3):
            window = shifted[
                :, :, offset_z : offset_z + count_z, offset_y : offset_y + count_y
            ]
            summed = summed + jnp.einsum(
                "oce,cezyx->ozyx",
                conv_weight[:, :, offset_z, offset_y, :],
                window,
                preferred_element_type=jnp.float32,
            )
    return summed


def extend(cells, width):
    for axis, dim in (("gz", 1), ("yx", 2)):
        size = cells.shape[dim]
        head = lax.slice_in_dim(cells, 0, width, axis=dim)
        tail = lax.slice_in_dim(cells, size - width, size, axis=dim)
        cells = jnp.concatenate(
            [from_behind(tail, axis, 1), cells, from_behind(head, axis, -1)], axis=dim
        )
    return cells


def operator_cells(grid):
    weight_zup, weight_yup, weight_x, seeded = grid
    inner = slice(1, weight_zup.shape[0] - 1)
    lower = slice(0, weight_zup.shape[0] - 2)
    weight_xup = weight_x[inner, inner]
    weight_xdown = jnp.pad(weight_xup, ((0, 0), (0, 0), (1, 0)))[:, :, :-1]
    edges = (
        weight_zup[inner, inner],
        weight_zup[lower, inner],
        weight_yup[inner, inner],
        weight_yup[inner, lower],
        weight_xup,
        weight_xdown,
    )
    mask = seeded[inner, inner]
    free = 1.0 - mask
    total = edges[0] + edges[1] + edges[2] + edges[3] + edges[4] + edges[5]
    diagonal = free * (total + RIDGE_WEIGHT) + mask
    return diagonal, tuple(free * edge for edge in edges)


def operate_inside(field, cells, offset):
    diagonal, edges = cells
    count = field.shape[1] - 2
    part = slice(offset - 1, offset - 1 + count)
    centre = field[:, 1:-1, 1:-1]
    zero_col = jnp.zeros_like(centre[..., :1])
    near = (
        field[:, 2:, 1:-1],
        field[:, :-2, 1:-1],
        field[:, 1:-1, 2:],
        field[:, 1:-1, :-2],
        jnp.concatenate([centre[..., 1:], zero_col], axis=3),
        jnp.concatenate([zero_col, centre[..., :-1]], axis=3),
    )
    coupled = edges[0][part, part] * near[0]
    for edge, value in zip(edges[1:], near[1:]):
        coupled = coupled + edge[part, part] * value
    return diagonal[part, part] * centre - coupled


def all_sum(value, axes):
    for axis in axes:
        devices = lax.axis_size(axis)
        if devices & (devices - 1):
            value = lax.psum(value, axis)
            continue
        hop = 1
        while hop < devices:
            value = value + lax.ppermute(value, axis, [(i, i ^ hop) for i in range(devices)])
            hop *= 2
    return value


def field_sums(left, right):
    return jnp.sum(left * right, axis=(1, 2, 3))


def body(features, conv_weight, conv_bias, labels):
    depth_cells = features.shape[1]
    row_cells = features.shape[2]
    col_cells = features.shape[3]
    global_z = lax.axis_index("gz") * depth_cells + jnp.arange(depth_cells, dtype=jnp.int32)
    global_y = lax.axis_index("yx") * row_cells + jnp.arange(row_cells, dtype=jnp.int32)
    keep_z = (global_z < depth_cells * lax.axis_size("gz") - 1).astype(jnp.float32)[:, None, None]
    keep_y = (global_y < row_cells * lax.axis_size("yx") - 1).astype(jnp.float32)[None, :, None]
    keep_x = (jnp.arange(col_cells, dtype=jnp.int32) < col_cells - 1).astype(jnp.float32)[
        None, None, :
    ]
    bias_column = conv_bias[:, None, None, None]
    padded = padded_2(features, (("gz", 1), ("yx", 2)), 1)
    padded = jnp.pad(padded, ((0, 0), (0, 0), (0, 0), (1, 1)))
    affinities = jax.nn.sigmoid(
        conv_region(padded, conv_weight, depth_cells, row_cells) + bias_column
    )
    halo = ITERS + 1
    stacked = jnp.concatenate([affinities, labels[None].astype(jnp.float32)], axis=0)
    grid_cells = extend(stacked, halo)
    cells_z = depth_cells + 2 * halo
    cells_y = row_cells + 2 * halo
    grid_z = lax.axis_index("gz") * depth_cells - halo + jnp.arange(cells_z, dtype=jnp.int32)
    grid_y = lax.axis_index("yx") * row_cells - halo + jnp.arange(cells_y, dtype=jnp.int32)
    edge_z = ((grid_z >= 0) & (grid_z < depth_cells * lax.axis_size("gz") - 1)).astype(jnp.float32)
    edge_y = ((grid_y >= 0) & (grid_y < row_cells * lax.axis_size("yx") - 1)).astype(jnp.float32)
    grid_labels = grid_cells[3]
    grid = (
        grid_cells[0] * edge_z[:, None, None],
        grid_cells[1] * edge_y[None, :, None],
        grid_cells[2] * keep_x,
        (grid_labels > 0.5).astype(jnp.float32),
    )
    colours = jnp.arange(1, FIELDS + 1, dtype=jnp.float32)[:, None, None, None]
    grid_seed = (grid_labels[None] == colours).astype(jnp.float32)
    seed_field = grid_seed[:, halo:-halo, halo:-halo]

    inside = grid_seed[:, 1:-1, 1:-1]
    cells = operator_cells(grid)
    current = inside - operate_inside(grid_seed, cells, 1)
    basis = [current]
    for power in range(ITERS):
        current = operate_inside(current, cells, power + 2)
        basis.append(current)
    basis = [
        vector[:, (vector.shape[1] - depth_cells) // 2 : (vector.shape[1] + depth_cells) // 2,
               (vector.shape[2] - row_cells) // 2 : (vector.shape[2] + row_cells) // 2]
        for vector in basis
    ]
    size = ITERS + 1
    pairs = [(i, j) for i in range(size) for j in range(i, size) if i < size - 1]
    local = jnp.stack([field_sums(basis[i], basis[j]) for i, j in pairs])
    total = all_sum(local, ("gz", "yx"))
    gram = {}
    for index, (i, j) in enumerate(pairs):
        gram[i, j] = total[index]
        gram[j, i] = total[index]

    zero = jnp.zeros((FIELDS,), jnp.float32)
    one = jnp.ones((FIELDS,), jnp.float32)

    def inner(left, right):
        acc = zero
        for i in range(size):
            for j in range(size):
                if (i, j) in gram and not (
                    isinstance(left[i], float) or isinstance(right[j], float)
                ):
                    acc = acc + left[i] * gram[i, j] * right[j]
        return acc

    def shift(coeffs):
        return [0.0] + coeffs[:-1]

    def axpy(scale, left, right):
        out = []
        for a, b in zip(left, right):
            if isinstance(b, float):
                out.append(a)
            elif isinstance(a, float):
                out.append(scale * b)
            else:
                out.append(a + scale * b)
        return out

    residual = [one] + [0.0] * (size - 1)
    direction = list(residual)
    solution = [0.0] * size
    norm_now = inner(residual, residual)
    for iteration in range(ITERS):
        applied = shift(direction)
        step_size = norm_now / inner(direction, applied)
        solution = axpy(step_size, solution, direction)
        if iteration == ITERS - 1:
            break
        residual = axpy(-step_size, residual, applied)
        norm_next = inner(residual, residual)
        direction = axpy(norm_next / norm_now, residual, direction)
        norm_now = norm_next

    probabilities = seed_field
    for coeff, vector in zip(solution, basis):
        if not isinstance(coeff, float):
            probabilities = probabilities + coeff[:, None, None, None] * vector
    return (probabilities, affinities)


def solution(mesh):
    in_specs = (P(None, "gz", "yx", None), P(), P(), P("gz", "yx", None))
    out_specs = (P(None, "gz", "yx", None), P(None, "gz", "yx", None))
    return jax.shard_map(body, mesh=mesh, in_specs=in_specs, out_specs=out_specs, check_vma=False)
```

```python
import jax
import jax.numpy as jnp
from jax import lax
from jax.sharding import PartitionSpec as P

FIELDS = 8
ITERS = 3


RIDGE_WEIGHT = 0.5


def padded_2(cells, sides, width):
    for axis, dim in sides:
        count = lax.axis_size(axis)
        ends = count - 1
        head = lax.slice_in_dim(cells, 0, width, axis=dim)
        tail = lax.slice_in_dim(cells, cells.shape[dim] - width, cells.shape[dim], axis=dim)
        cells = jnp.concatenate(
            [
                lax.ppermute(tail, axis, [(i, (i + 1) % count) for i in range(ends)]),
                cells,
                lax.ppermute(head, axis, [((i + 1) % count, i) for i in range(ends)]),
            ],
            axis=dim,
        )
    return cells


def from_behind(value, axis, by):
    devices = lax.axis_size(axis)
    pairs = [(i, i + by) for i in range(devices) if 0 <= i + by < devices]
    return lax.ppermute(value, axis, pairs)


def conv_region(padded, conv_weight, count_z, count_y):
    col_cells = padded.shape[3] - 2
    shifted = jnp.stack(
        [padded[..., offset_x : offset_x + col_cells] for offset_x in range(3)], axis=1
    )
    summed = jnp.zeros((3, count_z, count_y, col_cells), jnp.float32)
    for offset_z in range(3):
        for offset_y in range(3):
            window = shifted[
                :, :, offset_z : offset_z + count_z, offset_y : offset_y + count_y
            ]
            summed = summed + jnp.einsum(
                "oce,cezyx->ozyx",
                conv_weight[:, :, offset_z, offset_y, :],
                window,
                preferred_element_type=jnp.float32,
            )
    return summed


def extend(cells, width):
    for axis, dim in (("gz", 1), ("yx", 2)):
        size = cells.shape[dim]
        head = lax.slice_in_dim(cells, 0, width, axis=dim)
        tail = lax.slice_in_dim(cells, size - width, size, axis=dim)
        cells = jnp.concatenate(
            [from_behind(tail, axis, 1), cells, from_behind(head, axis, -1)], axis=dim
        )
    return cells


def operator_cells(grid):
    weight_zup, weight_yup, weight_x, seeded = grid
    inner = slice(1, weight_zup.shape[0] - 1)
    lower = slice(0, weight_zup.shape[0] - 2)
    weight_xup = weight_x[inner, inner]
    weight_xdown = jnp.pad(weight_xup, ((0, 0), (0, 0), (1, 0)))[:, :, :-1]
    edges = (
        weight_zup[inner, inner],
        weight_zup[lower, inner],
        weight_yup[inner, inner],
        weight_yup[inner, lower],
        weight_xup,
        weight_xdown,
    )
    mask = seeded[inner, inner]
    free = 1.0 - mask
    total = edges[0] + edges[1] + edges[2] + edges[3] + edges[4] + edges[5]
    diagonal = free * (total + RIDGE_WEIGHT) + mask
    return diagonal, tuple(free * edge for edge in edges)


def operate_inside(field, cells, offset):
    diagonal, edges = cells
    count = field.shape[1] - 2
    part = slice(offset - 1, offset - 1 + count)
    centre = field[:, 1:-1, 1:-1]
    zero_col = jnp.zeros_like(centre[..., :1])
    near = (
        field[:, 2:, 1:-1],
        field[:, :-2, 1:-1],
        field[:, 1:-1, 2:],
        field[:, 1:-1, :-2],
        jnp.concatenate([centre[..., 1:], zero_col], axis=3),
        jnp.concatenate([zero_col, centre[..., :-1]], axis=3),
    )
    coupled = edges[0][part, part] * near[0]
    for edge, value in zip(edges[1:], near[1:]):
        coupled = coupled + edge[part, part] * value
    return diagonal[part, part] * centre - coupled


def all_sum(value, axes):
    for axis in axes:
        devices = lax.axis_size(axis)
        if devices & (devices - 1):
            value = lax.psum(value, axis)
            continue
        hop = 1
        while hop < devices:
            value = value + lax.ppermute(value, axis, [(i, i ^ hop) for i in range(devices)])
            hop *= 2
    return value


def field_sums(left, right):
    return jnp.sum(left * right, axis=(1, 2, 3))


def body(features, conv_weight, conv_bias, labels):
    depth_cells = features.shape[1]
    row_cells = features.shape[2]
    col_cells = features.shape[3]
    global_z = lax.axis_index("gz") * depth_cells + jnp.arange(depth_cells, dtype=jnp.int32)
    global_y = lax.axis_index("yx") * row_cells + jnp.arange(row_cells, dtype=jnp.int32)
    keep_z = (global_z < depth_cells * lax.axis_size("gz") - 1).astype(jnp.float32)[:, None, None]
    keep_y = (global_y < row_cells * lax.axis_size("yx") - 1).astype(jnp.float32)[None, :, None]
    keep_x = (jnp.arange(col_cells, dtype=jnp.int32) < col_cells - 1).astype(jnp.float32)[
        None, None, :
    ]
    halo = ITERS + 1
    channels = features.shape[0]
    stacked = jnp.concatenate([features, labels[None].astype(features.dtype)], axis=0)
    grid_cells = extend(stacked, halo + 1)
    padded = jnp.pad(grid_cells[:channels], ((0, 0), (0, 0), (0, 0), (1, 1)))
    cells_z = depth_cells + 2 * halo
    cells_y = row_cells + 2 * halo
    grid_aff = jax.nn.sigmoid(
        conv_region(padded, conv_weight, cells_z, cells_y) + conv_bias[:, None, None, None]
    )
    affinities = grid_aff[:, halo:-halo, halo:-halo]
    grid_labels = grid_cells[channels, 1:-1, 1:-1].astype(jnp.float32)
    grid_z = lax.axis_index("gz") * depth_cells - halo + jnp.arange(cells_z, dtype=jnp.int32)
    grid_y = lax.axis_index("yx") * row_cells - halo + jnp.arange(cells_y, dtype=jnp.int32)
    edge_z = ((grid_z >= 0) & (grid_z < depth_cells * lax.axis_size("gz") - 1)).astype(jnp.float32)
    edge_y = ((grid_y >= 0) & (grid_y < row_cells * lax.axis_size("yx") - 1)).astype(jnp.float32)
    grid = (
        grid_aff[0] * edge_z[:, None, None],
        grid_aff[1] * edge_y[None, :, None],
        grid_aff[2] * keep_x,
        (grid_labels > 0.5).astype(jnp.float32),
    )
    colours = jnp.arange(1, FIELDS + 1, dtype=jnp.float32)[:, None, None, None]
    grid_seed = (grid_labels[None] == colours).astype(jnp.float32)
    seed_field = grid_seed[:, halo:-halo, halo:-halo]

    inside = grid_seed[:, 1:-1, 1:-1]
    cells = operator_cells(grid)
    current = inside - operate_inside(grid_seed, cells, 1)
    basis = [current]
    for power in range(ITERS):
        current = operate_inside(current, cells, power + 2)
        basis.append(current)
    basis = [
        vector[:, (vector.shape[1] - depth_cells) // 2 : (vector.shape[1] + depth_cells) // 2,
               (vector.shape[2] - row_cells) // 2 : (vector.shape[2] + row_cells) // 2]
        for vector in basis
    ]
    size = ITERS + 1
    pairs = [(i, j) for i in range(size) for j in range(i, size) if i < size - 1]
    local = jnp.stack([field_sums(basis[i], basis[j]) for i, j in pairs])
    total = all_sum(local, ("gz", "yx"))
    gram = {}
    for index, (i, j) in enumerate(pairs):
        gram[i, j] = total[index]
        gram[j, i] = total[index]

    zero = jnp.zeros((FIELDS,), jnp.float32)
    one = jnp.ones((FIELDS,), jnp.float32)

    def inner(left, right):
        acc = zero
        for i in range(size):
            for j in range(size):
                if (i, j) in gram and not (
                    isinstance(left[i], float) or isinstance(right[j], float)
                ):
                    acc = acc + left[i] * gram[i, j] * right[j]
        return acc

    def shift(coeffs):
        return [0.0] + coeffs[:-1]

    def axpy(scale, left, right):
        out = []
        for a, b in zip(left, right):
            if isinstance(b, float):
                out.append(a)
            elif isinstance(a, float):
                out.append(scale * b)
            else:
                out.append(a + scale * b)
        return out

    residual = [one] + [0.0] * (size - 1)
    direction = list(residual)
    solution = [0.0] * size
    norm_now = inner(residual, residual)
    for iteration in range(ITERS):
        applied = shift(direction)
        step_size = norm_now / inner(direction, applied)
        solution = axpy(step_size, solution, direction)
        if iteration == ITERS - 1:
            break
        residual = axpy(-step_size, residual, applied)
        norm_next = inner(residual, residual)
        direction = axpy(norm_next / norm_now, residual, direction)
        norm_now = norm_next

    probabilities = seed_field
    for coeff, vector in zip(solution, basis):
        if not isinstance(coeff, float):
            probabilities = probabilities + coeff[:, None, None, None] * vector
    return (probabilities, affinities)


def solution(mesh):
    in_specs = (P(None, "gz", "yx", None), P(), P(), P("gz", "yx", None))
    out_specs = (P(None, "gz", "yx", None), P(None, "gz", "yx", None))
    return jax.shard_map(body, mesh=mesh, in_specs=in_specs, out_specs=out_specs, check_vma=False)
```

```python
import jax
import jax.numpy as jnp
from jax import lax
from jax.sharding import PartitionSpec as P

FIELDS = 8
ITERS = 3


RIDGE_WEIGHT = 0.5


def padded_2(cells, sides, width):
    for axis, dim in sides:
        count = lax.axis_size(axis)
        ends = count - 1
        head = lax.slice_in_dim(cells, 0, width, axis=dim)
        tail = lax.slice_in_dim(cells, cells.shape[dim] - width, cells.shape[dim], axis=dim)
        cells = jnp.concatenate(
            [
                lax.ppermute(tail, axis, [(i, (i + 1) % count) for i in range(ends)]),
                cells,
                lax.ppermute(head, axis, [((i + 1) % count, i) for i in range(ends)]),
            ],
            axis=dim,
        )
    return cells


def from_behind(value, axis, by):
    devices = lax.axis_size(axis)
    pairs = [(i, i + by) for i in range(devices) if 0 <= i + by < devices]
    return lax.ppermute(value, axis, pairs)


def conv_region(padded, conv_weight, count_z, count_y):
    col_cells = padded.shape[3] - 2
    shifted = jnp.stack(
        [padded[..., offset_x : offset_x + col_cells] for offset_x in range(3)], axis=1
    )
    summed = jnp.zeros((3, count_z, count_y, col_cells), jnp.float32)
    for offset_z in range(3):
        for offset_y in range(3):
            window = shifted[
                :, :, offset_z : offset_z + count_z, offset_y : offset_y + count_y
            ]
            summed = summed + jnp.einsum(
                "oce,cezyx->ozyx",
                conv_weight[:, :, offset_z, offset_y, :],
                window,
                preferred_element_type=jnp.float32,
            )
    return summed


def from_ring(value, axis, by):
    devices = lax.axis_size(axis)
    moved = lax.ppermute(value, axis, [(i, (i + by) % devices) for i in range(devices)])
    source = lax.axis_index(axis) - by
    inside = (source >= 0) & (source < devices)
    return jnp.where(inside, moved, jnp.zeros_like(moved))


def extend(cells, width):
    for axis, dim in (("gz", 1), ("yx", 2)):
        size = cells.shape[dim]
        head = lax.slice_in_dim(cells, 0, width, axis=dim)
        tail = lax.slice_in_dim(cells, size - width, size, axis=dim)
        cells = jnp.concatenate(
            [from_ring(tail, axis, 1), cells, from_ring(head, axis, -1)], axis=dim
        )
    return cells


def operator_cells(grid):
    weight_zup, weight_yup, weight_x, seeded = grid
    inner = slice(1, weight_zup.shape[0] - 1)
    lower = slice(0, weight_zup.shape[0] - 2)
    weight_xup = weight_x[inner, inner]
    weight_xdown = jnp.pad(weight_xup, ((0, 0), (0, 0), (1, 0)))[:, :, :-1]
    edges = (
        weight_zup[inner, inner],
        weight_zup[lower, inner],
        weight_yup[inner, inner],
        weight_yup[inner, lower],
        weight_xup,
        weight_xdown,
    )
    mask = seeded[inner, inner]
    free = 1.0 - mask
    total = edges[0] + edges[1] + edges[2] + edges[3] + edges[4] + edges[5]
    diagonal = free * (total + RIDGE_WEIGHT) + mask
    return diagonal, tuple(free * edge for edge in edges)


def operate_inside(field, cells, offset):
    diagonal, edges = cells
    count = field.shape[1] - 2
    part = slice(offset - 1, offset - 1 + count)
    centre = field[:, 1:-1, 1:-1]
    zero_col = jnp.zeros_like(centre[..., :1])
    near = (
        field[:, 2:, 1:-1],
        field[:, :-2, 1:-1],
        field[:, 1:-1, 2:],
        field[:, 1:-1, :-2],
        jnp.concatenate([centre[..., 1:], zero_col], axis=3),
        jnp.concatenate([zero_col, centre[..., :-1]], axis=3),
    )
    coupled = edges[0][part, part] * near[0]
    for edge, value in zip(edges[1:], near[1:]):
        coupled = coupled + edge[part, part] * value
    return diagonal[part, part] * centre - coupled


def all_sum(value, axes):
    for axis in axes:
        devices = lax.axis_size(axis)
        if devices & (devices - 1):
            value = lax.psum(value, axis)
            continue
        hop = 1
        while hop < devices:
            value = value + lax.ppermute(value, axis, [(i, i ^ hop) for i in range(devices)])
            hop *= 2
    return value


def field_sums(left, right):
    return jnp.sum(left * right, axis=(1, 2, 3))


def body(features, conv_weight, conv_bias, labels):
    depth_cells = features.shape[1]
    row_cells = features.shape[2]
    col_cells = features.shape[3]
    global_z = lax.axis_index("gz") * depth_cells + jnp.arange(depth_cells, dtype=jnp.int32)
    global_y = lax.axis_index("yx") * row_cells + jnp.arange(row_cells, dtype=jnp.int32)
    keep_z = (global_z < depth_cells * lax.axis_size("gz") - 1).astype(jnp.float32)[:, None, None]
    keep_y = (global_y < row_cells * lax.axis_size("yx") - 1).astype(jnp.float32)[None, :, None]
    keep_x = (jnp.arange(col_cells, dtype=jnp.int32) < col_cells - 1).astype(jnp.float32)[
        None, None, :
    ]
    bias_column = conv_bias[:, None, None, None]
    padded = extend(features, 1)
    padded = jnp.pad(padded, ((0, 0), (0, 0), (0, 0), (1, 1)))
    affinities = jax.nn.sigmoid(
        conv_region(padded, conv_weight, depth_cells, row_cells) + bias_column
    )
    halo = ITERS + 1
    stacked = jnp.concatenate([affinities, labels[None].astype(jnp.float32)], axis=0)
    grid_cells = extend(stacked, halo)
    cells_z = depth_cells + 2 * halo
    cells_y = row_cells + 2 * halo
    grid_z = lax.axis_index("gz") * depth_cells - halo + jnp.arange(cells_z, dtype=jnp.int32)
    grid_y = lax.axis_index("yx") * row_cells - halo + jnp.arange(cells_y, dtype=jnp.int32)
    edge_z = ((grid_z >= 0) & (grid_z < depth_cells * lax.axis_size("gz") - 1)).astype(jnp.float32)
    edge_y = ((grid_y >= 0) & (grid_y < row_cells * lax.axis_size("yx") - 1)).astype(jnp.float32)
    grid_labels = grid_cells[3]
    grid = (
        grid_cells[0] * edge_z[:, None, None],
        grid_cells[1] * edge_y[None, :, None],
        grid_cells[2] * keep_x,
        (grid_labels > 0.5).astype(jnp.float32),
    )
    colours = jnp.arange(1, FIELDS + 1, dtype=jnp.float32)[:, None, None, None]
    grid_seed = (grid_labels[None] == colours).astype(jnp.float32)
    seed_field = grid_seed[:, halo:-halo, halo:-halo]

    inside = grid_seed[:, 1:-1, 1:-1]
    cells = operator_cells(grid)
    current = inside - operate_inside(grid_seed, cells, 1)
    basis = [current]
    for power in range(ITERS):
        current = operate_inside(current, cells, power + 2)
        basis.append(current)
    basis = [
        vector[:, (vector.shape[1] - depth_cells) // 2 : (vector.shape[1] + depth_cells) // 2,
               (vector.shape[2] - row_cells) // 2 : (vector.shape[2] + row_cells) // 2]
        for vector in basis
    ]
    size = ITERS + 1
    pairs = [(i, j) for i in range(size) for j in range(i, size) if i < size - 1]
    local = jnp.stack([field_sums(basis[i], basis[j]) for i, j in pairs])
    total = all_sum(local, ("gz", "yx"))
    gram = {}
    for index, (i, j) in enumerate(pairs):
        gram[i, j] = total[index]
        gram[j, i] = total[index]

    zero = jnp.zeros((FIELDS,), jnp.float32)
    one = jnp.ones((FIELDS,), jnp.float32)

    def inner(left, right):
        acc = zero
        for i in range(size):
            for j in range(size):
                if (i, j) in gram and not (
                    isinstance(left[i], float) or isinstance(right[j], float)
                ):
                    acc = acc + left[i] * gram[i, j] * right[j]
        return acc

    def shift(coeffs):
        return [0.0] + coeffs[:-1]

    def axpy(scale, left, right):
        out = []
        for a, b in zip(left, right):
            if isinstance(b, float):
                out.append(a)
            elif isinstance(a, float):
                out.append(scale * b)
            else:
                out.append(a + scale * b)
        return out

    residual = [one] + [0.0] * (size - 1)
    direction = list(residual)
    solution = [0.0] * size
    norm_now = inner(residual, residual)
    for iteration in range(ITERS):
        applied = shift(direction)
        step_size = norm_now / inner(direction, applied)
        solution = axpy(step_size, solution, direction)
        if iteration == ITERS - 1:
            break
        residual = axpy(-step_size, residual, applied)
        norm_next = inner(residual, residual)
        direction = axpy(norm_next / norm_now, residual, direction)
        norm_now = norm_next

    probabilities = seed_field
    for coeff, vector in zip(solution, basis):
        if not isinstance(coeff, float):
            probabilities = probabilities + coeff[:, None, None, None] * vector
    return (probabilities, affinities)


def solution(mesh):
    in_specs = (P(None, "gz", "yx", None), P(), P(), P("gz", "yx", None))
    out_specs = (P(None, "gz", "yx", None), P(None, "gz", "yx", None))
    return jax.shard_map(body, mesh=mesh, in_specs=in_specs, out_specs=out_specs, check_vma=False)
```

```python
import jax
import jax.numpy as jnp
from jax import lax
from jax.sharding import PartitionSpec as P

FIELDS = 8
ITERS = 3


RIDGE_WEIGHT = 0.5


def padded_2(cells, sides, width):
    for axis, dim in sides:
        count = lax.axis_size(axis)
        ends = count - 1
        head = lax.slice_in_dim(cells, 0, width, axis=dim)
        tail = lax.slice_in_dim(cells, cells.shape[dim] - width, cells.shape[dim], axis=dim)
        cells = jnp.concatenate(
            [
                lax.ppermute(tail, axis, [(i, (i + 1) % count) for i in range(ends)]),
                cells,
                lax.ppermute(head, axis, [((i + 1) % count, i) for i in range(ends)]),
            ],
            axis=dim,
        )
    return cells


def from_behind(value, axis, by):
    devices = lax.axis_size(axis)
    pairs = [(i, i + by) for i in range(devices) if 0 <= i + by < devices]
    return lax.ppermute(value, axis, pairs)


def conv_region(padded, conv_weight, count_z, count_y):
    col_cells = padded.shape[3] - 2
    shifted = jnp.stack(
        [padded[..., offset_x : offset_x + col_cells] for offset_x in range(3)], axis=1
    )
    summed = jnp.zeros((3, count_z, count_y, col_cells), jnp.float32)
    for offset_z in range(3):
        for offset_y in range(3):
            window = shifted[
                :, :, offset_z : offset_z + count_z, offset_y : offset_y + count_y
            ]
            summed = summed + jnp.einsum(
                "oce,cezyx->ozyx",
                conv_weight[:, :, offset_z, offset_y, :],
                window,
                preferred_element_type=jnp.float32,
            )
    return summed


def from_ring(value, axis, by):
    devices = lax.axis_size(axis)
    moved = lax.ppermute(value, axis, [(i, (i + by) % devices) for i in range(devices)])
    source = lax.axis_index(axis) - by
    inside = (source >= 0) & (source < devices)
    return jnp.where(inside, moved, jnp.zeros_like(moved))


def extend(cells, width):
    for axis, dim in (("gz", 1), ("yx", 2)):
        size = cells.shape[dim]
        head = lax.slice_in_dim(cells, 0, width, axis=dim)
        tail = lax.slice_in_dim(cells, size - width, size, axis=dim)
        cells = jnp.concatenate(
            [from_ring(tail, axis, 1), cells, from_ring(head, axis, -1)], axis=dim
        )
    return cells


def operator_cells(grid):
    weight_zup, weight_yup, weight_x, seeded = grid
    inner = slice(1, weight_zup.shape[0] - 1)
    lower = slice(0, weight_zup.shape[0] - 2)
    weight_xup = weight_x[inner, inner]
    weight_xdown = jnp.pad(weight_xup, ((0, 0), (0, 0), (1, 0)))[:, :, :-1]
    edges = (
        weight_zup[inner, inner],
        weight_zup[lower, inner],
        weight_yup[inner, inner],
        weight_yup[inner, lower],
        weight_xup,
        weight_xdown,
    )
    mask = seeded[inner, inner]
    free = 1.0 - mask
    total = edges[0] + edges[1] + edges[2] + edges[3] + edges[4] + edges[5]
    diagonal = free * (total + RIDGE_WEIGHT) + mask
    return diagonal, tuple(free * edge for edge in edges)


def operate_inside(field, cells, offset):
    diagonal, edges = cells
    count = field.shape[1] - 2
    part = slice(offset - 1, offset - 1 + count)
    centre = field[:, 1:-1, 1:-1]
    zero_col = jnp.zeros_like(centre[..., :1])
    near = (
        field[:, 2:, 1:-1],
        field[:, :-2, 1:-1],
        field[:, 1:-1, 2:],
        field[:, 1:-1, :-2],
        jnp.concatenate([centre[..., 1:], zero_col], axis=3),
        jnp.concatenate([zero_col, centre[..., :-1]], axis=3),
    )
    coupled = edges[0][part, part] * near[0]
    for edge, value in zip(edges[1:], near[1:]):
        coupled = coupled + edge[part, part] * value
    return diagonal[part, part] * centre - coupled


def all_sum(value, axes):
    for axis in axes:
        devices = lax.axis_size(axis)
        if devices & (devices - 1):
            value = lax.psum(value, axis)
            continue
        hop = 1
        while hop < devices:
            value = value + lax.ppermute(value, axis, [(i, i ^ hop) for i in range(devices)])
            hop *= 2
    return value


def field_sums(left, right):
    return jnp.sum(left * right, axis=(1, 2, 3))


def body(features, conv_weight, conv_bias, labels):
    depth_cells = features.shape[1]
    row_cells = features.shape[2]
    col_cells = features.shape[3]
    global_z = lax.axis_index("gz") * depth_cells + jnp.arange(depth_cells, dtype=jnp.int32)
    global_y = lax.axis_index("yx") * row_cells + jnp.arange(row_cells, dtype=jnp.int32)
    keep_z = (global_z < depth_cells * lax.axis_size("gz") - 1).astype(jnp.float32)[:, None, None]
    keep_y = (global_y < row_cells * lax.axis_size("yx") - 1).astype(jnp.float32)[None, :, None]
    keep_x = (jnp.arange(col_cells, dtype=jnp.int32) < col_cells - 1).astype(jnp.float32)[
        None, None, :
    ]
    bias_column = conv_bias[:, None, None, None]
    padded = extend(features, 1)
    padded = jnp.pad(padded, ((0, 0), (0, 0), (0, 0), (1, 1)))
    affinities = jax.nn.sigmoid(
        conv_region(padded, conv_weight, depth_cells, row_cells) + bias_column
    )
    halo = ITERS + 1
    stacked = jnp.concatenate([affinities, labels[None].astype(jnp.float32)], axis=0)
    grid_cells = extend(stacked, halo)
    cells_z = depth_cells + 2 * halo
    cells_y = row_cells + 2 * halo
    grid_z = lax.axis_index("gz") * depth_cells - halo + jnp.arange(cells_z, dtype=jnp.int32)
    grid_y = lax.axis_index("yx") * row_cells - halo + jnp.arange(cells_y, dtype=jnp.int32)
    edge_z = ((grid_z >= 0) & (grid_z < depth_cells * lax.axis_size("gz") - 1)).astype(jnp.float32)
    edge_y = ((grid_y >= 0) & (grid_y < row_cells * lax.axis_size("yx") - 1)).astype(jnp.float32)
    grid_labels = grid_cells[3]
    grid = (
        grid_cells[0] * edge_z[:, None, None],
        grid_cells[1] * edge_y[None, :, None],
        grid_cells[2] * keep_x,
        (grid_labels > 0.5).astype(jnp.float32),
    )
    colours = jnp.arange(1, FIELDS + 1, dtype=jnp.float32)[:, None, None, None]
    grid_seed = (grid_labels[None] == colours).astype(jnp.float32)
    seed_field = (labels[None] == jnp.arange(1, FIELDS + 1, dtype=jnp.int32)[:, None, None, None]).astype(jnp.float32)

    inside = grid_seed[:, 1:-1, 1:-1]
    cells = operator_cells(grid)
    current = inside - operate_inside(grid_seed, cells, 1)
    basis = [current]
    for power in range(ITERS):
        current = operate_inside(current, cells, power + 2)
        basis.append(current)
    basis = [
        vector[:, (vector.shape[1] - depth_cells) // 2 : (vector.shape[1] + depth_cells) // 2,
               (vector.shape[2] - row_cells) // 2 : (vector.shape[2] + row_cells) // 2]
        for vector in basis
    ]
    size = ITERS + 1
    pairs = [(i, j) for i in range(size) for j in range(i, size) if i < size - 1]
    local = jnp.stack([field_sums(basis[i], basis[j]) for i, j in pairs])
    total = all_sum(local, ("gz", "yx"))
    gram = {}
    for index, (i, j) in enumerate(pairs):
        gram[i, j] = total[index]
        gram[j, i] = total[index]

    zero = jnp.zeros((FIELDS,), jnp.float32)
    one = jnp.ones((FIELDS,), jnp.float32)

    def inner(left, right):
        acc = zero
        for i in range(size):
            for j in range(size):
                if (i, j) in gram and not (
                    isinstance(left[i], float) or isinstance(right[j], float)
                ):
                    acc = acc + left[i] * gram[i, j] * right[j]
        return acc

    def shift(coeffs):
        return [0.0] + coeffs[:-1]

    def axpy(scale, left, right):
        out = []
        for a, b in zip(left, right):
            if isinstance(b, float):
                out.append(a)
            elif isinstance(a, float):
                out.append(scale * b)
            else:
                out.append(a + scale * b)
        return out

    residual = [one] + [0.0] * (size - 1)
    direction = list(residual)
    solution = [0.0] * size
    norm_now = inner(residual, residual)
    for iteration in range(ITERS):
        applied = shift(direction)
        step_size = norm_now / inner(direction, applied)
        solution = axpy(step_size, solution, direction)
        if iteration == ITERS - 1:
            break
        residual = axpy(-step_size, residual, applied)
        norm_next = inner(residual, residual)
        direction = axpy(norm_next / norm_now, residual, direction)
        norm_now = norm_next

    probabilities = seed_field
    for coeff, vector in zip(solution, basis):
        if not isinstance(coeff, float):
            probabilities = probabilities + coeff[:, None, None, None] * vector
    return (probabilities, affinities)


def solution(mesh):
    in_specs = (P(None, "gz", "yx", None), P(), P(), P("gz", "yx", None))
    out_specs = (P(None, "gz", "yx", None), P(None, "gz", "yx", None))
    return jax.shard_map(body, mesh=mesh, in_specs=in_specs, out_specs=out_specs, check_vma=False)
```

```python
import jax
import jax.numpy as jnp
from jax import lax
from jax.sharding import PartitionSpec as P

FIELDS = 8
ITERS = 3


RIDGE_WEIGHT = 0.5


def padded_2(cells, sides, width):
    for axis, dim in sides:
        count = lax.axis_size(axis)
        ends = count - 1
        head = lax.slice_in_dim(cells, 0, width, axis=dim)
        tail = lax.slice_in_dim(cells, cells.shape[dim] - width, cells.shape[dim], axis=dim)
        cells = jnp.concatenate(
            [
                lax.ppermute(tail, axis, [(i, (i + 1) % count) for i in range(ends)]),
                cells,
                lax.ppermute(head, axis, [((i + 1) % count, i) for i in range(ends)]),
            ],
            axis=dim,
        )
    return cells


def from_behind(value, axis, by):
    devices = lax.axis_size(axis)
    pairs = [(i, i + by) for i in range(devices) if 0 <= i + by < devices]
    return lax.ppermute(value, axis, pairs)


def conv_region(padded, conv_weight, count_z, count_y):
    col_cells = padded.shape[3] - 2
    shifted = jnp.stack(
        [padded[..., offset_x : offset_x + col_cells] for offset_x in range(3)], axis=1
    )
    summed = jnp.zeros((3, count_z, count_y, col_cells), jnp.float32)
    for offset_z in range(3):
        for offset_y in range(3):
            window = shifted[
                :, :, offset_z : offset_z + count_z, offset_y : offset_y + count_y
            ]
            summed = summed + jnp.einsum(
                "oce,cezyx->ozyx",
                conv_weight[:, :, offset_z, offset_y, :],
                window,
                preferred_element_type=jnp.float32,
            )
    return summed


def from_ring(value, axis, by):
    devices = lax.axis_size(axis)
    moved = lax.ppermute(value, axis, [(i, (i + by) % devices) for i in range(devices)])
    source = lax.axis_index(axis) - by
    inside = (source >= 0) & (source < devices)
    return jnp.where(inside, moved, jnp.zeros_like(moved))


def extend(cells, width):
    for axis, dim in (("gz", 1), ("yx", 2)):
        size = cells.shape[dim]
        head = lax.slice_in_dim(cells, 0, width, axis=dim)
        tail = lax.slice_in_dim(cells, size - width, size, axis=dim)
        cells = jnp.concatenate(
            [from_ring(tail, axis, 1), cells, from_ring(head, axis, -1)], axis=dim
        )
    return cells


def operator_cells(grid):
    weight_zup, weight_yup, weight_x, seeded = grid
    inner = slice(1, weight_zup.shape[0] - 1)
    lower = slice(0, weight_zup.shape[0] - 2)
    weight_xup = weight_x[inner, inner]
    weight_xdown = jnp.pad(weight_xup, ((0, 0), (0, 0), (1, 0)))[:, :, :-1]
    edges = (
        weight_zup[inner, inner],
        weight_zup[lower, inner],
        weight_yup[inner, inner],
        weight_yup[inner, lower],
        weight_xup,
        weight_xdown,
    )
    mask = seeded[inner, inner]
    free = 1.0 - mask
    total = edges[0] + edges[1] + edges[2] + edges[3] + edges[4] + edges[5]
    diagonal = free * (total + RIDGE_WEIGHT) + mask
    return diagonal, tuple(free * edge for edge in edges)


def operate_inside(field, cells, offset):
    diagonal, edges = cells
    count = field.shape[1] - 2
    part = slice(offset - 1, offset - 1 + count)
    centre = field[:, 1:-1, 1:-1]
    zero_col = jnp.zeros_like(centre[..., :1])
    near = (
        field[:, 2:, 1:-1],
        field[:, :-2, 1:-1],
        field[:, 1:-1, 2:],
        field[:, 1:-1, :-2],
        jnp.concatenate([centre[..., 1:], zero_col], axis=3),
        jnp.concatenate([zero_col, centre[..., :-1]], axis=3),
    )
    coupled = edges[0][part, part] * near[0]
    for edge, value in zip(edges[1:], near[1:]):
        coupled = coupled + edge[part, part] * value
    return diagonal[part, part] * centre - coupled


def all_sum(value, axes):
    for axis in axes:
        devices = lax.axis_size(axis)
        if devices & (devices - 1):
            value = lax.psum(value, axis)
            continue
        hop = 1
        while hop < devices:
            value = value + lax.ppermute(value, axis, [(i, i ^ hop) for i in range(devices)])
            hop *= 2
    return value


def field_sums(left, right):
    return jnp.sum(left * right, axis=(1, 2, 3))


def body(features, conv_weight, conv_bias, labels):
    depth_cells = features.shape[1]
    row_cells = features.shape[2]
    col_cells = features.shape[3]
    global_z = lax.axis_index("gz") * depth_cells + jnp.arange(depth_cells, dtype=jnp.int32)
    global_y = lax.axis_index("yx") * row_cells + jnp.arange(row_cells, dtype=jnp.int32)
    keep_z = (global_z < depth_cells * lax.axis_size("gz") - 1).astype(jnp.float32)[:, None, None]
    keep_y = (global_y < row_cells * lax.axis_size("yx") - 1).astype(jnp.float32)[None, :, None]
    keep_x = (jnp.arange(col_cells, dtype=jnp.int32) < col_cells - 1).astype(jnp.float32)[
        None, None, :
    ]
    bias_column = conv_bias[:, None, None, None]
    padded = extend(features, 1)
    padded = jnp.pad(padded, ((0, 0), (0, 0), (0, 0), (1, 1)))
    affinities = jax.nn.sigmoid(
        conv_region(padded, conv_weight, depth_cells, row_cells) + bias_column
    )
    halo = ITERS + 1
    stacked = jnp.concatenate([affinities, labels[None].astype(jnp.float32)], axis=0)
    grid_cells = extend(stacked, halo)
    cells_z = depth_cells + 2 * halo
    cells_y = row_cells + 2 * halo
    grid_z = lax.axis_index("gz") * depth_cells - halo + jnp.arange(cells_z, dtype=jnp.int32)
    grid_y = lax.axis_index("yx") * row_cells - halo + jnp.arange(cells_y, dtype=jnp.int32)
    edge_z = ((grid_z >= 0) & (grid_z < depth_cells * lax.axis_size("gz") - 1)).astype(jnp.float32)
    edge_y = ((grid_y >= 0) & (grid_y < row_cells * lax.axis_size("yx") - 1)).astype(jnp.float32)
    grid_labels = grid_cells[3]
    grid = (
        grid_cells[0] * edge_z[:, None, None],
        grid_cells[1] * edge_y[None, :, None],
        grid_cells[2] * keep_x,
        (grid_labels > 0.5).astype(jnp.float32),
    )
    colours = jnp.arange(1, FIELDS + 1, dtype=jnp.float32)[:, None, None, None]
    grid_seed = (grid_labels[None] == colours).astype(jnp.float32)
    seed_field = (labels[None] == jnp.arange(1, FIELDS + 1, dtype=jnp.int32)[:, None, None, None]).astype(jnp.float32)

    cells = operator_cells(grid)

    def solve(grid_seed, seed_field):
        count = seed_field.shape[0]
        inside = grid_seed[:, 1:-1, 1:-1]
        current = inside - operate_inside(grid_seed, cells, 1)
        basis = [current]
        for power in range(ITERS):
            current = operate_inside(current, cells, power + 2)
            basis.append(current)
        basis = [
            vector[:, (vector.shape[1] - depth_cells) // 2 : (vector.shape[1] + depth_cells) // 2,
                   (vector.shape[2] - row_cells) // 2 : (vector.shape[2] + row_cells) // 2]
            for vector in basis
        ]
        size = ITERS + 1
        pairs = [(i, j) for i in range(size) for j in range(i, size) if i < size - 1]
        local = jnp.stack([field_sums(basis[i], basis[j]) for i, j in pairs])
        total = all_sum(local, ("gz", "yx"))
        gram = {}
        for index, (i, j) in enumerate(pairs):
            gram[i, j] = total[index]
            gram[j, i] = total[index]

        zero = jnp.zeros((count,), jnp.float32)
        one = jnp.ones((count,), jnp.float32)

        def inner(left, right):
            acc = zero
            for i in range(size):
                for j in range(size):
                    if (i, j) in gram and not (
                        isinstance(left[i], float) or isinstance(right[j], float)
                    ):
                        acc = acc + left[i] * gram[i, j] * right[j]
            return acc

        def shift(coeffs):
            return [0.0] + coeffs[:-1]

        def axpy(scale, left, right):
            out = []
            for a, b in zip(left, right):
                if isinstance(b, float):
                    out.append(a)
                elif isinstance(a, float):
                    out.append(scale * b)
                else:
                    out.append(a + scale * b)
            return out

        residual = [one] + [0.0] * (size - 1)
        direction = list(residual)
        solution = [0.0] * size
        norm_now = inner(residual, residual)
        for iteration in range(ITERS):
            applied = shift(direction)
            step_size = norm_now / inner(direction, applied)
            solution = axpy(step_size, solution, direction)
            if iteration == ITERS - 1:
                break
            residual = axpy(-step_size, residual, applied)
            norm_next = inner(residual, residual)
            direction = axpy(norm_next / norm_now, residual, direction)
            norm_now = norm_next

        probabilities = seed_field
        for coeff, vector in zip(solution, basis):
            if not isinstance(coeff, float):
                probabilities = probabilities + coeff[:, None, None, None] * vector
        return probabilities

    half = FIELDS // 2
    probabilities = jnp.concatenate(
        [solve(grid_seed[:half], seed_field[:half]), solve(grid_seed[half:], seed_field[half:])],
        axis=0,
    )
    return (probabilities, affinities)


def solution(mesh):
    in_specs = (P(None, "gz", "yx", None), P(), P(), P("gz", "yx", None))
    out_specs = (P(None, "gz", "yx", None), P(None, "gz", "yx", None))
    return jax.shard_map(body, mesh=mesh, in_specs=in_specs, out_specs=out_specs, check_vma=False)
```

```python
import jax
import jax.numpy as jnp
from jax import lax
from jax.sharding import PartitionSpec as P

FIELDS = 8
ITERS = 3


RIDGE_WEIGHT = 0.5


def padded_2(cells, sides, width):
    for axis, dim in sides:
        count = lax.axis_size(axis)
        ends = count - 1
        head = lax.slice_in_dim(cells, 0, width, axis=dim)
        tail = lax.slice_in_dim(cells, cells.shape[dim] - width, cells.shape[dim], axis=dim)
        cells = jnp.concatenate(
            [
                lax.ppermute(tail, axis, [(i, (i + 1) % count) for i in range(ends)]),
                cells,
                lax.ppermute(head, axis, [((i + 1) % count, i) for i in range(ends)]),
            ],
            axis=dim,
        )
    return cells


def from_behind(value, axis, by):
    devices = lax.axis_size(axis)
    pairs = [(i, i + by) for i in range(devices) if 0 <= i + by < devices]
    return lax.ppermute(value, axis, pairs)


def conv_region(padded, conv_weight, count_z, count_y):
    col_cells = padded.shape[3] - 2
    shifted = jnp.stack(
        [padded[..., offset_x : offset_x + col_cells] for offset_x in range(3)], axis=1
    )
    summed = jnp.zeros((3, count_z, count_y, col_cells), jnp.float32)
    for offset_z in range(3):
        for offset_y in range(3):
            window = shifted[
                :, :, offset_z : offset_z + count_z, offset_y : offset_y + count_y
            ]
            summed = summed + jnp.einsum(
                "oce,cezyx->ozyx",
                conv_weight[:, :, offset_z, offset_y, :],
                window,
                preferred_element_type=jnp.float32,
            )
    return summed


def from_ring(value, axis, by):
    devices = lax.axis_size(axis)
    moved = lax.ppermute(value, axis, [(i, (i + by) % devices) for i in range(devices)])
    source = lax.axis_index(axis) - by
    inside = (source >= 0) & (source < devices)
    return jnp.where(inside, moved, jnp.zeros_like(moved))


def extend(cells, width, corner=None):
    corner = width if corner is None else corner
    for axis, dim in (("gz", 1), ("yx", 2)):
        source = cells
        trim = 0
        if dim == 2 and corner < width:
            trim = width - corner
            source = cells[:, trim : cells.shape[1] - trim]
        size = source.shape[dim]
        head = lax.slice_in_dim(source, 0, width, axis=dim)
        tail = lax.slice_in_dim(source, size - width, size, axis=dim)
        edges = [from_ring(tail, axis, 1), from_ring(head, axis, -1)]
        if trim:
            edges = [jnp.pad(edge, ((0, 0), (trim, trim), (0, 0), (0, 0))) for edge in edges]
        cells = jnp.concatenate([edges[0], cells, edges[1]], axis=dim)
    return cells


def operator_cells(grid):
    weight_zup, weight_yup, weight_x, seeded = grid
    inner = slice(1, weight_zup.shape[0] - 1)
    lower = slice(0, weight_zup.shape[0] - 2)
    weight_xup = weight_x[inner, inner]
    weight_xdown = jnp.pad(weight_xup, ((0, 0), (0, 0), (1, 0)))[:, :, :-1]
    edges = (
        weight_zup[inner, inner],
        weight_zup[lower, inner],
        weight_yup[inner, inner],
        weight_yup[inner, lower],
        weight_xup,
        weight_xdown,
    )
    mask = seeded[inner, inner]
    free = 1.0 - mask
    total = edges[0] + edges[1] + edges[2] + edges[3] + edges[4] + edges[5]
    diagonal = free * (total + RIDGE_WEIGHT) + mask
    return diagonal, tuple(free * edge for edge in edges)


def operate_inside(field, cells, offset):
    diagonal, edges = cells
    count = field.shape[1] - 2
    part = slice(offset - 1, offset - 1 + count)
    centre = field[:, 1:-1, 1:-1]
    zero_col = jnp.zeros_like(centre[..., :1])
    near = (
        field[:, 2:, 1:-1],
        field[:, :-2, 1:-1],
        field[:, 1:-1, 2:],
        field[:, 1:-1, :-2],
        jnp.concatenate([centre[..., 1:], zero_col], axis=3),
        jnp.concatenate([zero_col, centre[..., :-1]], axis=3),
    )
    coupled = edges[0][part, part] * near[0]
    for edge, value in zip(edges[1:], near[1:]):
        coupled = coupled + edge[part, part] * value
    return diagonal[part, part] * centre - coupled


def all_sum(value, axes):
    for axis in axes:
        devices = lax.axis_size(axis)
        if devices & (devices - 1):
            value = lax.psum(value, axis)
            continue
        hop = 1
        while hop < devices:
            value = value + lax.ppermute(value, axis, [(i, i ^ hop) for i in range(devices)])
            hop *= 2
    return value


def field_sums(left, right):
    return jnp.sum(left * right, axis=(1, 2, 3))


def body(features, conv_weight, conv_bias, labels):
    depth_cells = features.shape[1]
    row_cells = features.shape[2]
    col_cells = features.shape[3]
    global_z = lax.axis_index("gz") * depth_cells + jnp.arange(depth_cells, dtype=jnp.int32)
    global_y = lax.axis_index("yx") * row_cells + jnp.arange(row_cells, dtype=jnp.int32)
    keep_z = (global_z < depth_cells * lax.axis_size("gz") - 1).astype(jnp.float32)[:, None, None]
    keep_y = (global_y < row_cells * lax.axis_size("yx") - 1).astype(jnp.float32)[None, :, None]
    keep_x = (jnp.arange(col_cells, dtype=jnp.int32) < col_cells - 1).astype(jnp.float32)[
        None, None, :
    ]
    bias_column = conv_bias[:, None, None, None]
    padded = extend(features, 1)
    padded = jnp.pad(padded, ((0, 0), (0, 0), (0, 0), (1, 1)))
    affinities = jax.nn.sigmoid(
        conv_region(padded, conv_weight, depth_cells, row_cells) + bias_column
    )
    halo = ITERS + 1
    stacked = jnp.concatenate([affinities, labels[None].astype(jnp.float32)], axis=0)
    grid_cells = extend(stacked, halo, halo - 1)
    cells_z = depth_cells + 2 * halo
    cells_y = row_cells + 2 * halo
    grid_z = lax.axis_index("gz") * depth_cells - halo + jnp.arange(cells_z, dtype=jnp.int32)
    grid_y = lax.axis_index("yx") * row_cells - halo + jnp.arange(cells_y, dtype=jnp.int32)
    edge_z = ((grid_z >= 0) & (grid_z < depth_cells * lax.axis_size("gz") - 1)).astype(jnp.float32)
    edge_y = ((grid_y >= 0) & (grid_y < row_cells * lax.axis_size("yx") - 1)).astype(jnp.float32)
    grid_labels = grid_cells[3]
    grid = (
        grid_cells[0] * edge_z[:, None, None],
        grid_cells[1] * edge_y[None, :, None],
        grid_cells[2] * keep_x,
        (grid_labels > 0.5).astype(jnp.float32),
    )
    colours = jnp.arange(1, FIELDS + 1, dtype=jnp.float32)[:, None, None, None]
    grid_seed = (grid_labels[None] == colours).astype(jnp.float32)
    seed_field = (labels[None] == jnp.arange(1, FIELDS + 1, dtype=jnp.int32)[:, None, None, None]).astype(jnp.float32)

    inside = grid_seed[:, 1:-1, 1:-1]
    cells = operator_cells(grid)
    current = inside - operate_inside(grid_seed, cells, 1)
    basis = [current]
    for power in range(ITERS):
        current = operate_inside(current, cells, power + 2)
        basis.append(current)
    basis = [
        vector[:, (vector.shape[1] - depth_cells) // 2 : (vector.shape[1] + depth_cells) // 2,
               (vector.shape[2] - row_cells) // 2 : (vector.shape[2] + row_cells) // 2]
        for vector in basis
    ]
    size = ITERS + 1
    pairs = [(i, j) for i in range(size) for j in range(i, size) if i < size - 1]
    local = jnp.stack([field_sums(basis[i], basis[j]) for i, j in pairs])
    total = all_sum(local, ("gz", "yx"))
    gram = {}
    for index, (i, j) in enumerate(pairs):
        gram[i, j] = total[index]
        gram[j, i] = total[index]

    zero = jnp.zeros((FIELDS,), jnp.float32)
    one = jnp.ones((FIELDS,), jnp.float32)

    def inner(left, right):
        acc = zero
        for i in range(size):
            for j in range(size):
                if (i, j) in gram and not (
                    isinstance(left[i], float) or isinstance(right[j], float)
                ):
                    acc = acc + left[i] * gram[i, j] * right[j]
        return acc

    def shift(coeffs):
        return [0.0] + coeffs[:-1]

    def axpy(scale, left, right):
        out = []
        for a, b in zip(left, right):
            if isinstance(b, float):
                out.append(a)
            elif isinstance(a, float):
                out.append(scale * b)
            else:
                out.append(a + scale * b)
        return out

    residual = [one] + [0.0] * (size - 1)
    direction = list(residual)
    solution = [0.0] * size
    norm_now = inner(residual, residual)
    for iteration in range(ITERS):
        applied = shift(direction)
        step_size = norm_now / inner(direction, applied)
        solution = axpy(step_size, solution, direction)
        if iteration == ITERS - 1:
            break
        residual = axpy(-step_size, residual, applied)
        norm_next = inner(residual, residual)
        direction = axpy(norm_next / norm_now, residual, direction)
        norm_now = norm_next

    probabilities = seed_field
    for coeff, vector in zip(solution, basis):
        if not isinstance(coeff, float):
            probabilities = probabilities + coeff[:, None, None, None] * vector
    return (probabilities, affinities)


def solution(mesh):
    in_specs = (P(None, "gz", "yx", None), P(), P(), P("gz", "yx", None))
    out_specs = (P(None, "gz", "yx", None), P(None, "gz", "yx", None))
    return jax.shard_map(body, mesh=mesh, in_specs=in_specs, out_specs=out_specs, check_vma=False)
```

```python
import jax
import jax.numpy as jnp
from jax import lax
from jax.sharding import PartitionSpec as P

FIELDS = 8
ITERS = 3


RIDGE_WEIGHT = 0.5


def padded_2(cells, sides, width):
    for axis, dim in sides:
        count = lax.axis_size(axis)
        ends = count - 1
        head = lax.slice_in_dim(cells, 0, width, axis=dim)
        tail = lax.slice_in_dim(cells, cells.shape[dim] - width, cells.shape[dim], axis=dim)
        cells = jnp.concatenate(
            [
                lax.ppermute(tail, axis, [(i, (i + 1) % count) for i in range(ends)]),
                cells,
                lax.ppermute(head, axis, [((i + 1) % count, i) for i in range(ends)]),
            ],
            axis=dim,
        )
    return cells


def from_behind(value, axis, by):
    devices = lax.axis_size(axis)
    pairs = [(i, i + by) for i in range(devices) if 0 <= i + by < devices]
    return lax.ppermute(value, axis, pairs)


def conv_region(padded, conv_weight, count_z, count_y):
    col_cells = padded.shape[3] - 2
    shifted = jnp.stack(
        [padded[..., offset_x : offset_x + col_cells] for offset_x in range(3)], axis=1
    )
    summed = jnp.zeros((3, count_z, count_y, col_cells), jnp.float32)
    for offset_z in range(3):
        for offset_y in range(3):
            window = shifted[
                :, :, offset_z : offset_z + count_z, offset_y : offset_y + count_y
            ]
            summed = summed + jnp.einsum(
                "oce,cezyx->ozyx",
                conv_weight[:, :, offset_z, offset_y, :],
                window,
                preferred_element_type=jnp.float32,
            )
    return summed


def from_ring(value, axis, by):
    devices = lax.axis_size(axis)
    moved = lax.ppermute(value, axis, [(i, (i + by) % devices) for i in range(devices)])
    source = lax.axis_index(axis) - by
    inside = (source >= 0) & (source < devices)
    return jnp.where(inside, moved, jnp.zeros_like(moved))


def extend(cells, width, corner=None, order=(("gz", 1), ("yx", 2))):
    corner = width if corner is None else corner
    for step, (axis, dim) in enumerate(order):
        source = cells
        trim = 0
        if step == 1 and corner < width:
            trim = width - corner
            other = order[0][1]
            source = lax.slice_in_dim(cells, trim, cells.shape[other] - trim, axis=other)
        size = source.shape[dim]
        head = lax.slice_in_dim(source, 0, width, axis=dim)
        tail = lax.slice_in_dim(source, size - width, size, axis=dim)
        edges = [from_ring(tail, axis, 1), from_ring(head, axis, -1)]
        if trim:
            pads = [(0, 0)] * 4
            pads[other] = (trim, trim)
            edges = [jnp.pad(edge, pads) for edge in edges]
        cells = jnp.concatenate([edges[0], cells, edges[1]], axis=dim)
    return cells


def operator_cells(grid):
    weight_zup, weight_yup, weight_x, seeded = grid
    inner = slice(1, weight_zup.shape[0] - 1)
    lower = slice(0, weight_zup.shape[0] - 2)
    weight_xup = weight_x[inner, inner]
    weight_xdown = jnp.pad(weight_xup, ((0, 0), (0, 0), (1, 0)))[:, :, :-1]
    edges = (
        weight_zup[inner, inner],
        weight_zup[lower, inner],
        weight_yup[inner, inner],
        weight_yup[inner, lower],
        weight_xup,
        weight_xdown,
    )
    mask = seeded[inner, inner]
    free = 1.0 - mask
    total = edges[0] + edges[1] + edges[2] + edges[3] + edges[4] + edges[5]
    diagonal = free * (total + RIDGE_WEIGHT) + mask
    return diagonal, tuple(free * edge for edge in edges)


def operate_inside(field, cells, offset):
    diagonal, edges = cells
    count = field.shape[1] - 2
    part = slice(offset - 1, offset - 1 + count)
    centre = field[:, 1:-1, 1:-1]
    zero_col = jnp.zeros_like(centre[..., :1])
    near = (
        field[:, 2:, 1:-1],
        field[:, :-2, 1:-1],
        field[:, 1:-1, 2:],
        field[:, 1:-1, :-2],
        jnp.concatenate([centre[..., 1:], zero_col], axis=3),
        jnp.concatenate([zero_col, centre[..., :-1]], axis=3),
    )
    coupled = edges[0][part, part] * near[0]
    for edge, value in zip(edges[1:], near[1:]):
        coupled = coupled + edge[part, part] * value
    return diagonal[part, part] * centre - coupled


def all_sum(value, axes):
    for axis in axes:
        devices = lax.axis_size(axis)
        if devices & (devices - 1):
            value = lax.psum(value, axis)
            continue
        hop = 1
        while hop < devices:
            value = value + lax.ppermute(value, axis, [(i, i ^ hop) for i in range(devices)])
            hop *= 2
    return value


def field_sums(left, right):
    return jnp.sum(left * right, axis=(1, 2, 3))


def body(features, conv_weight, conv_bias, labels):
    depth_cells = features.shape[1]
    row_cells = features.shape[2]
    col_cells = features.shape[3]
    global_z = lax.axis_index("gz") * depth_cells + jnp.arange(depth_cells, dtype=jnp.int32)
    global_y = lax.axis_index("yx") * row_cells + jnp.arange(row_cells, dtype=jnp.int32)
    keep_z = (global_z < depth_cells * lax.axis_size("gz") - 1).astype(jnp.float32)[:, None, None]
    keep_y = (global_y < row_cells * lax.axis_size("yx") - 1).astype(jnp.float32)[None, :, None]
    keep_x = (jnp.arange(col_cells, dtype=jnp.int32) < col_cells - 1).astype(jnp.float32)[
        None, None, :
    ]
    bias_column = conv_bias[:, None, None, None]
    padded = extend(features, 1)
    padded = jnp.pad(padded, ((0, 0), (0, 0), (0, 0), (1, 1)))
    affinities = jax.nn.sigmoid(
        conv_region(padded, conv_weight, depth_cells, row_cells) + bias_column
    )
    halo = ITERS + 1
    stacked = jnp.concatenate([affinities, labels[None].astype(jnp.float32)], axis=0)
    grid_cells = extend(stacked, halo, halo - 1, (("yx", 2), ("gz", 1)))
    cells_z = depth_cells + 2 * halo
    cells_y = row_cells + 2 * halo
    grid_z = lax.axis_index("gz") * depth_cells - halo + jnp.arange(cells_z, dtype=jnp.int32)
    grid_y = lax.axis_index("yx") * row_cells - halo + jnp.arange(cells_y, dtype=jnp.int32)
    edge_z = ((grid_z >= 0) & (grid_z < depth_cells * lax.axis_size("gz") - 1)).astype(jnp.float32)
    edge_y = ((grid_y >= 0) & (grid_y < row_cells * lax.axis_size("yx") - 1)).astype(jnp.float32)
    grid_labels = grid_cells[3]
    grid = (
        grid_cells[0] * edge_z[:, None, None],
        grid_cells[1] * edge_y[None, :, None],
        grid_cells[2] * keep_x,
        (grid_labels > 0.5).astype(jnp.float32),
    )
    colours = jnp.arange(1, FIELDS + 1, dtype=jnp.float32)[:, None, None, None]
    grid_seed = (grid_labels[None] == colours).astype(jnp.float32)
    seed_field = (labels[None] == jnp.arange(1, FIELDS + 1, dtype=jnp.int32)[:, None, None, None]).astype(jnp.float32)

    inside = grid_seed[:, 1:-1, 1:-1]
    cells = operator_cells(grid)
    current = inside - operate_inside(grid_seed, cells, 1)
    basis = [current]
    for power in range(ITERS):
        current = operate_inside(current, cells, power + 2)
        basis.append(current)
    basis = [
        vector[:, (vector.shape[1] - depth_cells) // 2 : (vector.shape[1] + depth_cells) // 2,
               (vector.shape[2] - row_cells) // 2 : (vector.shape[2] + row_cells) // 2]
        for vector in basis
    ]
    size = ITERS + 1
    pairs = [(i, j) for i in range(size) for j in range(i, size) if i < size - 1]
    local = jnp.stack([field_sums(basis[i], basis[j]) for i, j in pairs])
    total = all_sum(local, ("gz", "yx"))
    gram = {}
    for index, (i, j) in enumerate(pairs):
        gram[i, j] = total[index]
        gram[j, i] = total[index]

    zero = jnp.zeros((FIELDS,), jnp.float32)
    one = jnp.ones((FIELDS,), jnp.float32)

    def inner(left, right):
        acc = zero
        for i in range(size):
            for j in range(size):
                if (i, j) in gram and not (
                    isinstance(left[i], float) or isinstance(right[j], float)
                ):
                    acc = acc + left[i] * gram[i, j] * right[j]
        return acc

    def shift(coeffs):
        return [0.0] + coeffs[:-1]

    def axpy(scale, left, right):
        out = []
        for a, b in zip(left, right):
            if isinstance(b, float):
                out.append(a)
            elif isinstance(a, float):
                out.append(scale * b)
            else:
                out.append(a + scale * b)
        return out

    residual = [one] + [0.0] * (size - 1)
    direction = list(residual)
    solution = [0.0] * size
    norm_now = inner(residual, residual)
    for iteration in range(ITERS):
        applied = shift(direction)
        step_size = norm_now / inner(direction, applied)
        solution = axpy(step_size, solution, direction)
        if iteration == ITERS - 1:
            break
        residual = axpy(-step_size, residual, applied)
        norm_next = inner(residual, residual)
        direction = axpy(norm_next / norm_now, residual, direction)
        norm_now = norm_next

    probabilities = seed_field
    for coeff, vector in zip(solution, basis):
        if not isinstance(coeff, float):
            probabilities = probabilities + coeff[:, None, None, None] * vector
    return (probabilities, affinities)


def solution(mesh):
    in_specs = (P(None, "gz", "yx", None), P(), P(), P("gz", "yx", None))
    out_specs = (P(None, "gz", "yx", None), P(None, "gz", "yx", None))
    return jax.shard_map(body, mesh=mesh, in_specs=in_specs, out_specs=out_specs, check_vma=False)
```

```python
import jax
import jax.numpy as jnp
from jax import lax
from jax.sharding import PartitionSpec as P

FIELDS = 8
ITERS = 3


RIDGE_WEIGHT = 0.5


def padded_2(cells, sides, width):
    for axis, dim in sides:
        count = lax.axis_size(axis)
        ends = count - 1
        head = lax.slice_in_dim(cells, 0, width, axis=dim)
        tail = lax.slice_in_dim(cells, cells.shape[dim] - width, cells.shape[dim], axis=dim)
        cells = jnp.concatenate(
            [
                lax.ppermute(tail, axis, [(i, (i + 1) % count) for i in range(ends)]),
                cells,
                lax.ppermute(head, axis, [((i + 1) % count, i) for i in range(ends)]),
            ],
            axis=dim,
        )
    return cells


def from_behind(value, axis, by):
    devices = lax.axis_size(axis)
    pairs = [(i, i + by) for i in range(devices) if 0 <= i + by < devices]
    return lax.ppermute(value, axis, pairs)


def conv_region(padded, conv_weight, count_z, count_y):
    col_cells = padded.shape[3] - 2
    shifted = jnp.stack(
        [padded[..., offset_x : offset_x + col_cells] for offset_x in range(3)], axis=1
    )
    summed = jnp.zeros((3, count_z, count_y, col_cells), jnp.float32)
    for offset_z in range(3):
        for offset_y in range(3):
            window = shifted[
                :, :, offset_z : offset_z + count_z, offset_y : offset_y + count_y
            ]
            summed = summed + jnp.einsum(
                "oce,cezyx->ozyx",
                conv_weight[:, :, offset_z, offset_y, :],
                window,
                preferred_element_type=jnp.float32,
            )
    return summed


def from_ring(value, axis, by):
    devices = lax.axis_size(axis)
    moved = lax.ppermute(value, axis, [(i, (i + by) % devices) for i in range(devices)])
    source = lax.axis_index(axis) - by
    inside = (source >= 0) & (source < devices)
    return jnp.where(inside, moved, jnp.zeros_like(moved))


def extend(cells, width, corner=None, order=(("gz", 1), ("yx", 2))):
    corner = width if corner is None else corner
    for step, (axis, dim) in enumerate(order):
        source = cells
        trim = 0
        if step == 1 and corner < width:
            trim = width - corner
            other = order[0][1]
            source = lax.slice_in_dim(cells, trim, cells.shape[other] - trim, axis=other)
        size = source.shape[dim]
        head = lax.slice_in_dim(source, 0, width, axis=dim)
        tail = lax.slice_in_dim(source, size - width, size, axis=dim)
        edges = [from_ring(tail, axis, 1), from_ring(head, axis, -1)]
        if trim:
            pads = [(0, 0)] * 4
            pads[other] = (trim, trim)
            edges = [jnp.pad(edge, pads) for edge in edges]
        cells = jnp.concatenate([edges[0], cells, edges[1]], axis=dim)
    return cells


def operator_cells(grid):
    weight_zup, weight_yup, weight_x, seeded = grid
    inner = slice(1, weight_zup.shape[0] - 1)
    lower = slice(0, weight_zup.shape[0] - 2)
    weight_xup = weight_x[inner, inner]
    weight_xdown = jnp.pad(weight_xup, ((0, 0), (0, 0), (1, 0)))[:, :, :-1]
    edges = (
        weight_zup[inner, inner],
        weight_zup[lower, inner],
        weight_yup[inner, inner],
        weight_yup[inner, lower],
        weight_xup,
        weight_xdown,
    )
    mask = seeded[inner, inner]
    free = 1.0 - mask
    total = edges[0] + edges[1] + edges[2] + edges[3] + edges[4] + edges[5]
    diagonal = free * (total + RIDGE_WEIGHT) + mask
    return diagonal, tuple(free * edge for edge in edges)


def operate_inside(field, cells, offset):
    diagonal, edges = cells
    count = field.shape[1] - 2
    part = slice(offset - 1, offset - 1 + count)
    centre = field[:, 1:-1, 1:-1]
    zero_col = jnp.zeros_like(centre[..., :1])
    near = (
        field[:, 2:, 1:-1],
        field[:, :-2, 1:-1],
        field[:, 1:-1, 2:],
        field[:, 1:-1, :-2],
        jnp.concatenate([centre[..., 1:], zero_col], axis=3),
        jnp.concatenate([zero_col, centre[..., :-1]], axis=3),
    )
    coupled = edges[0][part, part] * near[0]
    for edge, value in zip(edges[1:], near[1:]):
        coupled = coupled + edge[part, part] * value
    return diagonal[part, part] * centre - coupled


def all_sum(value, axes):
    for axis in axes:
        devices = lax.axis_size(axis)
        if devices & (devices - 1):
            value = lax.psum(value, axis)
            continue
        hop = 1
        while hop < devices:
            value = value + lax.ppermute(value, axis, [(i, i ^ hop) for i in range(devices)])
            hop *= 2
    return value


def field_sums(left, right):
    return jnp.sum(left * right, axis=(1, 2, 3))


def body(features, conv_weight, conv_bias, labels):
    depth_cells = features.shape[1]
    row_cells = features.shape[2]
    col_cells = features.shape[3]
    global_z = lax.axis_index("gz") * depth_cells + jnp.arange(depth_cells, dtype=jnp.int32)
    global_y = lax.axis_index("yx") * row_cells + jnp.arange(row_cells, dtype=jnp.int32)
    keep_z = (global_z < depth_cells * lax.axis_size("gz") - 1).astype(jnp.float32)[:, None, None]
    keep_y = (global_y < row_cells * lax.axis_size("yx") - 1).astype(jnp.float32)[None, :, None]
    keep_x = (jnp.arange(col_cells, dtype=jnp.int32) < col_cells - 1).astype(jnp.float32)[
        None, None, :
    ]
    bias_column = conv_bias[:, None, None, None]
    padded = extend(features, 1, order=(("yx", 2), ("gz", 1)))
    padded = jnp.pad(padded, ((0, 0), (0, 0), (0, 0), (1, 1)))
    affinities = jax.nn.sigmoid(
        conv_region(padded, conv_weight, depth_cells, row_cells) + bias_column
    )
    halo = ITERS + 1
    stacked = jnp.concatenate([affinities, labels[None].astype(jnp.float32)], axis=0)
    grid_cells = extend(stacked, halo, halo - 1, (("yx", 2), ("gz", 1)))
    cells_z = depth_cells + 2 * halo
    cells_y = row_cells + 2 * halo
    grid_z = lax.axis_index("gz") * depth_cells - halo + jnp.arange(cells_z, dtype=jnp.int32)
    grid_y = lax.axis_index("yx") * row_cells - halo + jnp.arange(cells_y, dtype=jnp.int32)
    edge_z = ((grid_z >= 0) & (grid_z < depth_cells * lax.axis_size("gz") - 1)).astype(jnp.float32)
    edge_y = ((grid_y >= 0) & (grid_y < row_cells * lax.axis_size("yx") - 1)).astype(jnp.float32)
    grid_labels = grid_cells[3]
    grid = (
        grid_cells[0] * edge_z[:, None, None],
        grid_cells[1] * edge_y[None, :, None],
        grid_cells[2] * keep_x,
        (grid_labels > 0.5).astype(jnp.float32),
    )
    colours = jnp.arange(1, FIELDS + 1, dtype=jnp.float32)[:, None, None, None]
    grid_seed = (grid_labels[None] == colours).astype(jnp.float32)
    seed_field = (labels[None] == jnp.arange(1, FIELDS + 1, dtype=jnp.int32)[:, None, None, None]).astype(jnp.float32)

    inside = grid_seed[:, 1:-1, 1:-1]
    cells = operator_cells(grid)
    current = inside - operate_inside(grid_seed, cells, 1)
    basis = [current]
    for power in range(ITERS):
        current = operate_inside(current, cells, power + 2)
        basis.append(current)
    basis = [
        vector[:, (vector.shape[1] - depth_cells) // 2 : (vector.shape[1] + depth_cells) // 2,
               (vector.shape[2] - row_cells) // 2 : (vector.shape[2] + row_cells) // 2]
        for vector in basis
    ]
    size = ITERS + 1
    pairs = [(i, j) for i in range(size) for j in range(i, size) if i < size - 1]
    local = jnp.stack([field_sums(basis[i], basis[j]) for i, j in pairs])
    total = all_sum(local, ("gz", "yx"))
    gram = {}
    for index, (i, j) in enumerate(pairs):
        gram[i, j] = total[index]
        gram[j, i] = total[index]

    zero = jnp.zeros((FIELDS,), jnp.float32)
    one = jnp.ones((FIELDS,), jnp.float32)

    def inner(left, right):
        acc = zero
        for i in range(size):
            for j in range(size):
                if (i, j) in gram and not (
                    isinstance(left[i], float) or isinstance(right[j], float)
                ):
                    acc = acc + left[i] * gram[i, j] * right[j]
        return acc

    def shift(coeffs):
        return [0.0] + coeffs[:-1]

    def axpy(scale, left, right):
        out = []
        for a, b in zip(left, right):
            if isinstance(b, float):
                out.append(a)
            elif isinstance(a, float):
                out.append(scale * b)
            else:
                out.append(a + scale * b)
        return out

    residual = [one] + [0.0] * (size - 1)
    direction = list(residual)
    solution = [0.0] * size
    norm_now = inner(residual, residual)
    for iteration in range(ITERS):
        applied = shift(direction)
        step_size = norm_now / inner(direction, applied)
        solution = axpy(step_size, solution, direction)
        if iteration == ITERS - 1:
            break
        residual = axpy(-step_size, residual, applied)
        norm_next = inner(residual, residual)
        direction = axpy(norm_next / norm_now, residual, direction)
        norm_now = norm_next

    probabilities = seed_field
    for coeff, vector in zip(solution, basis):
        if not isinstance(coeff, float):
            probabilities = probabilities + coeff[:, None, None, None] * vector
    return (probabilities, affinities)


def solution(mesh):
    in_specs = (P(None, "gz", "yx", None), P(), P(), P("gz", "yx", None))
    out_specs = (P(None, "gz", "yx", None), P(None, "gz", "yx", None))
    return jax.shard_map(body, mesh=mesh, in_specs=in_specs, out_specs=out_specs, check_vma=False)
```

```python
import jax
import jax.numpy as jnp
from jax import lax
from jax.sharding import PartitionSpec as P

FIELDS = 8
ITERS = 3


RIDGE_WEIGHT = 0.5


def padded_2(cells, sides, width):
    for axis, dim in sides:
        count = lax.axis_size(axis)
        ends = count - 1
        head = lax.slice_in_dim(cells, 0, width, axis=dim)
        tail = lax.slice_in_dim(cells, cells.shape[dim] - width, cells.shape[dim], axis=dim)
        cells = jnp.concatenate(
            [
                lax.ppermute(tail, axis, [(i, (i + 1) % count) for i in range(ends)]),
                cells,
                lax.ppermute(head, axis, [((i + 1) % count, i) for i in range(ends)]),
            ],
            axis=dim,
        )
    return cells


def from_behind(value, axis, by):
    devices = lax.axis_size(axis)
    pairs = [(i, i + by) for i in range(devices) if 0 <= i + by < devices]
    return lax.ppermute(value, axis, pairs)


def conv_region(padded, conv_weight, count_z, count_y):
    col_cells = padded.shape[3] - 2
    shifted = jnp.stack(
        [padded[..., offset_x : offset_x + col_cells] for offset_x in range(3)], axis=1
    )
    summed = jnp.zeros((3, count_z, count_y, col_cells), jnp.float32)
    for offset_z in range(3):
        for offset_y in range(3):
            window = shifted[
                :, :, offset_z : offset_z + count_z, offset_y : offset_y + count_y
            ]
            summed = summed + jnp.einsum(
                "oce,cezyx->ozyx",
                conv_weight[:, :, offset_z, offset_y, :],
                window,
                preferred_element_type=jnp.float32,
            )
    return summed


def from_ring(value, axis, by):
    devices = lax.axis_size(axis)
    moved = lax.ppermute(value, axis, [(i, (i + by) % devices) for i in range(devices)])
    source = lax.axis_index(axis) - by
    inside = (source >= 0) & (source < devices)
    return jnp.where(inside, moved, jnp.zeros_like(moved))


def extend(cells, width, corner=None, order=(("gz", 1), ("yx", 2)), first=0):
    corner = width if corner is None else corner
    for step, (axis, dim) in enumerate(order[: len(order) - first]):
        source = cells
        trim = 0
        if step + first == 1 and corner < width:
            trim = width - corner
            other = 3 - dim
            source = lax.slice_in_dim(cells, trim, cells.shape[other] - trim, axis=other)
        size = source.shape[dim]
        head = lax.slice_in_dim(source, 0, width, axis=dim)
        tail = lax.slice_in_dim(source, size - width, size, axis=dim)
        edges = [from_ring(tail, axis, 1), from_ring(head, axis, -1)]
        if trim:
            pads = [(0, 0)] * 4
            pads[other] = (trim, trim)
            edges = [jnp.pad(edge, pads) for edge in edges]
        cells = jnp.concatenate([edges[0], cells, edges[1]], axis=dim)
    return cells


def operator_cells(grid):
    weight_zup, weight_yup, weight_x, seeded = grid
    inner = slice(1, weight_zup.shape[0] - 1)
    lower = slice(0, weight_zup.shape[0] - 2)
    weight_xup = weight_x[inner, inner]
    weight_xdown = jnp.pad(weight_xup, ((0, 0), (0, 0), (1, 0)))[:, :, :-1]
    edges = (
        weight_zup[inner, inner],
        weight_zup[lower, inner],
        weight_yup[inner, inner],
        weight_yup[inner, lower],
        weight_xup,
        weight_xdown,
    )
    mask = seeded[inner, inner]
    free = 1.0 - mask
    total = edges[0] + edges[1] + edges[2] + edges[3] + edges[4] + edges[5]
    diagonal = free * (total + RIDGE_WEIGHT) + mask
    return diagonal, tuple(free * edge for edge in edges)


def operate_inside(field, cells, offset):
    diagonal, edges = cells
    count = field.shape[1] - 2
    part = slice(offset - 1, offset - 1 + count)
    centre = field[:, 1:-1, 1:-1]
    zero_col = jnp.zeros_like(centre[..., :1])
    near = (
        field[:, 2:, 1:-1],
        field[:, :-2, 1:-1],
        field[:, 1:-1, 2:],
        field[:, 1:-1, :-2],
        jnp.concatenate([centre[..., 1:], zero_col], axis=3),
        jnp.concatenate([zero_col, centre[..., :-1]], axis=3),
    )
    coupled = edges[0][part, part] * near[0]
    for edge, value in zip(edges[1:], near[1:]):
        coupled = coupled + edge[part, part] * value
    return diagonal[part, part] * centre - coupled


def all_sum(value, axes):
    for axis in axes:
        devices = lax.axis_size(axis)
        if devices & (devices - 1):
            value = lax.psum(value, axis)
            continue
        hop = 1
        while hop < devices:
            value = value + lax.ppermute(value, axis, [(i, i ^ hop) for i in range(devices)])
            hop *= 2
    return value


def field_sums(left, right):
    return jnp.sum(left * right, axis=(1, 2, 3))


def body(features, conv_weight, conv_bias, labels):
    depth_cells = features.shape[1]
    row_cells = features.shape[2]
    col_cells = features.shape[3]
    global_z = lax.axis_index("gz") * depth_cells + jnp.arange(depth_cells, dtype=jnp.int32)
    global_y = lax.axis_index("yx") * row_cells + jnp.arange(row_cells, dtype=jnp.int32)
    keep_z = (global_z < depth_cells * lax.axis_size("gz") - 1).astype(jnp.float32)[:, None, None]
    keep_y = (global_y < row_cells * lax.axis_size("yx") - 1).astype(jnp.float32)[None, :, None]
    keep_x = (jnp.arange(col_cells, dtype=jnp.int32) < col_cells - 1).astype(jnp.float32)[
        None, None, :
    ]
    bias_column = conv_bias[:, None, None, None]
    halo = ITERS + 1
    label_cells = labels[None].astype(jnp.float32)
    label_rows = jnp.concatenate(
        [
            from_ring(label_cells[:, :, row_cells - halo :], "yx", 1),
            label_cells,
            from_ring(label_cells[:, :, :halo], "yx", -1),
        ],
        axis=2,
    )
    padded = extend(features, 1)
    padded = jnp.pad(padded, ((0, 0), (0, 0), (0, 0), (1, 1)))
    affinities = jax.nn.sigmoid(
        conv_region(padded, conv_weight, depth_cells, row_cells) + bias_column
    )
    affinity_rows = jnp.concatenate(
        [
            from_ring(affinities[:, :, row_cells - halo :], "yx", 1),
            affinities,
            from_ring(affinities[:, :, :halo], "yx", -1),
        ],
        axis=2,
    )
    stacked = jnp.concatenate([affinity_rows, label_rows], axis=0)
    grid_cells = extend(stacked, halo, halo - 1, (("gz", 1), ("yx", 2)), first=1)
    cells_z = depth_cells + 2 * halo
    cells_y = row_cells + 2 * halo
    grid_z = lax.axis_index("gz") * depth_cells - halo + jnp.arange(cells_z, dtype=jnp.int32)
    grid_y = lax.axis_index("yx") * row_cells - halo + jnp.arange(cells_y, dtype=jnp.int32)
    edge_z = ((grid_z >= 0) & (grid_z < depth_cells * lax.axis_size("gz") - 1)).astype(jnp.float32)
    edge_y = ((grid_y >= 0) & (grid_y < row_cells * lax.axis_size("yx") - 1)).astype(jnp.float32)
    grid_labels = grid_cells[3]
    grid = (
        grid_cells[0] * edge_z[:, None, None],
        grid_cells[1] * edge_y[None, :, None],
        grid_cells[2] * keep_x,
        (grid_labels > 0.5).astype(jnp.float32),
    )
    colours = jnp.arange(1, FIELDS + 1, dtype=jnp.float32)[:, None, None, None]
    grid_seed = (grid_labels[None] == colours).astype(jnp.float32)
    seed_field = (labels[None] == jnp.arange(1, FIELDS + 1, dtype=jnp.int32)[:, None, None, None]).astype(jnp.float32)

    inside = grid_seed[:, 1:-1, 1:-1]
    cells = operator_cells(grid)
    current = inside - operate_inside(grid_seed, cells, 1)
    basis = [current]
    for power in range(ITERS):
        current = operate_inside(current, cells, power + 2)
        basis.append(current)
    basis = [
        vector[:, (vector.shape[1] - depth_cells) // 2 : (vector.shape[1] + depth_cells) // 2,
               (vector.shape[2] - row_cells) // 2 : (vector.shape[2] + row_cells) // 2]
        for vector in basis
    ]
    size = ITERS + 1
    pairs = [(i, j) for i in range(size) for j in range(i, size) if i < size - 1]
    local = jnp.stack([field_sums(basis[i], basis[j]) for i, j in pairs])
    total = all_sum(local, ("gz", "yx"))
    gram = {}
    for index, (i, j) in enumerate(pairs):
        gram[i, j] = total[index]
        gram[j, i] = total[index]

    zero = jnp.zeros((FIELDS,), jnp.float32)
    one = jnp.ones((FIELDS,), jnp.float32)

    def inner(left, right):
        acc = zero
        for i in range(size):
            for j in range(size):
                if (i, j) in gram and not (
                    isinstance(left[i], float) or isinstance(right[j], float)
                ):
                    acc = acc + left[i] * gram[i, j] * right[j]
        return acc

    def shift(coeffs):
        return [0.0] + coeffs[:-1]

    def axpy(scale, left, right):
        out = []
        for a, b in zip(left, right):
            if isinstance(b, float):
                out.append(a)
            elif isinstance(a, float):
                out.append(scale * b)
            else:
                out.append(a + scale * b)
        return out

    residual = [one] + [0.0] * (size - 1)
    direction = list(residual)
    solution = [0.0] * size
    norm_now = inner(residual, residual)
    for iteration in range(ITERS):
        applied = shift(direction)
        step_size = norm_now / inner(direction, applied)
        solution = axpy(step_size, solution, direction)
        if iteration == ITERS - 1:
            break
        residual = axpy(-step_size, residual, applied)
        norm_next = inner(residual, residual)
        direction = axpy(norm_next / norm_now, residual, direction)
        norm_now = norm_next

    probabilities = seed_field
    for coeff, vector in zip(solution, basis):
        if not isinstance(coeff, float):
            probabilities = probabilities + coeff[:, None, None, None] * vector
    return (probabilities, affinities)


def solution(mesh):
    in_specs = (P(None, "gz", "yx", None), P(), P(), P("gz", "yx", None))
    out_specs = (P(None, "gz", "yx", None), P(None, "gz", "yx", None))
    return jax.shard_map(body, mesh=mesh, in_specs=in_specs, out_specs=out_specs, check_vma=False)
```
